32 devices in a mesh: dp: 4 (over z), expert: 4 (over y, core), etp: 2 (over x).
Axes of the slice: x: 2, y: 2, z: 4, core: 2. Of those that a mesh axis runs over, the one named last changes fastest.
Arguments:
- grad_out: bfloat16 [2048, 4096], P(('dp', 'expert')), may hold values from -3 to 3
- routes: int32 [2048, 8], P(('dp', 'expert')), may hold values from 0 to 15, all different within a row; in each aligned block of 128 rows (0 to 127, 128 to 255, ...) at most 80 rows name the same one
- gates: bfloat16 [2048, 8], P(('dp', 'expert')), may hold values from 0.099609375 to 1
- hidden_saved: bfloat16 [4, 16, 320, 1536], P('dp', 'expert', None, 'etp'), may hold values from -1.5 to 1.5
- down_weight: bfloat16 [16, 1536, 4096], P('expert', 'etp', 'dp'), may hold values from -0.15625 to 0.15625
Outputs:
- weight_grad: bfloat16 [16, 1536, 4096], P('expert', 'etp', 'dp')
- hidden_grad: bfloat16 [4, 16, 320, 1536], P('dp', 'expert', None, 'etp')
- gate_grad: float32 [2048, 8], P(('dp', 'expert'))
The draws below stay inside these ranges and needn't reach their ends.
Inputs may be any that keep to these rules, and one draw needn't show every extreme that they name: `routes`: each row names 8 different experts. Within the rows of one device (aligned blocks of 128 rows) no expert is named more than 80 times, a bound that some block reaches.
All inputs are finite; a program needn't handle non-finite values.
Results may differ from the reference program's by a relative error of at most 0.005.
Values may be sent and summed in bfloat16 or wider, within the bound.
No kernel may reach another device: no remote copies, remote signals or barrier semaphores. Data moves between devices by JAX's collectives and lax.ppermute only.
A program may use at most 192 MiB of HBM per device.

```python
import math
import jax
import jax.numpy as jnp
import numpy as np
from jax import lax

D = 4096
FF = 1536
TOP = 8
TOK_DEV = 128
EXPERTS = 16
CAP = 80
TOKENS = 2048
N_DP = 4
N_EXPERT = 4


def block_scale(own_key, extent, shards, smallest, largest):
    gain, own = 1.0, jax.random.fold_in(own_key, 6)
    for position, blocks in shards:
        heights = jnp.exp(jax.random.uniform(jax.random.fold_in(own, position), (blocks,), jnp.float32, smallest / len(shards), largest / len(shards)))
        gain = gain * jnp.repeat(heights, extent[position] // blocks).reshape([-1 if axis == position else 1 for axis in range(len(extent))])
    return gain


def deal_out(stream_key, own, number, rows, number_of, top, reach, lean):
    order = jax.random.permutation(stream_key, number_of)
    packed, common = load_shares(number_of, rows * top, reach, lean, True), load_shares(number_of, rows * top, reach, lean, False)
    places = jnp.arange(number_of)

    def named(lengths, turn):
        used = int((lengths > 0).sum())
        fixed = max(1, used // 4)
        moved = fixed + (places - fixed + turn * (used - fixed)) % max(1, number_of - fixed)
        return jnp.zeros((number_of,), jnp.int32).at[order[jnp.where(places < fixed, places, moved)]].set(jnp.asarray(lengths, jnp.int32))

    lengths = jnp.where(number % 4 == 0, named(packed, number // 4), named(common, number - number // 4 - 1))
    mixed = jax.random.permutation(jax.random.fold_in(own, 3), number_of)
    source_of, receiver = mixed[0:number_of // 2 * 2:2], mixed[1:number_of // 2 * 2:2]
    room = jnp.minimum(lengths[source_of] - 1, reach - lengths[receiver]) // 2
    room = jnp.where((source_of == order[0]) | (receiver == order[0]) | (lengths[receiver] == 0), 0, jnp.maximum(room, 0))
    moved = jax.random.randint(jax.random.fold_in(own, 4), (number_of // 2,), 0, 1 << 20) % (room + 1)
    lengths = lengths.at[source_of].add(-moved).at[receiver].add(moved)
    labels = jnp.searchsorted(jnp.cumsum(lengths), jnp.arange(rows * top), side="right").astype(jnp.int32)
    grid = labels.reshape(top, rows).T
    grid = grid[jax.random.permutation(jax.random.fold_in(own, 1), rows)]
    turn = jax.random.randint(jax.random.fold_in(own, 2), (rows, 1), 0, top)
    return jnp.take_along_axis(grid, (jnp.arange(top)[None, :] + turn) % top, axis=1)


def load_shares(count, total, reach, slope, full):
    portions = [(1 << 20) // math.isqrt(grade ** slope) + 1 for grade in range(1, count + 1)]
    largest = reach if full else min(reach, max(-(-total // count), total * portions[0] // sum(portions)))
    least = 1 if total - largest >= count - 1 else 0
    holding, rest = [largest] + [least] * (count - 1), total - largest - least * (count - 1)
    while rest > 0:
        movable = [i for i in range(1, count) if holding[i] < largest] or [i for i in range(1, count) if holding[i] < reach]
        whole, budget = sum([portions[i] for i in movable]), rest
        for i in movable:
            extra = min(reach - holding[i], max(1, budget * portions[i] // whole), rest)
            holding[i] = holding[i] + extra
            rest = rest - extra
    return np.array(holding)


def centred(key, dims, deviation, bound, shards=(), held_as=jnp.bfloat16):
    values = jax.random.normal(key, dims, jnp.float32) * deviation
    if len(shards) > 0:
        values = block_scale(key, dims, shards, -0.22, 0.18) * values
    return jnp.clip(values, min=-bound, max=bound).astype(held_as)


def setup_inputs(seed: int = 0) -> dict:
    splits = jax.random.split(jax.random.key(seed), 6)
    grad_out = centred(splits[0], (TOKENS, D), 0.5, 3.0, ((0, 16),))
    routes_keys = jax.random.split(jax.random.fold_in(splits[1], 1), TOKENS // TOK_DEV)
    routes_turns = jax.random.permutation(jax.random.fold_in(splits[1], 3), TOKENS // TOK_DEV)
    routes = jax.vmap(lambda own, number: deal_out(jax.random.fold_in(splits[1], 2), own, number, TOK_DEV, EXPERTS, TOP, CAP, 2))(routes_keys, routes_turns).reshape((TOKENS, TOP))
    gates = jnp.clip(jnp.exp(math.log(1.0) - 2.306499 * jax.random.uniform(splits[2], (TOKENS, TOP), jnp.float32) ** block_scale(splits[2], (TOKENS, TOP), ((0, 16),), -0.2, 0.2)), 0.099609375, 1.0).astype(jnp.bfloat16)
    hidden_saved = centred(splits[3], (N_DP, EXPERTS, N_EXPERT * CAP, FF), 0.25, 1.5, ((0, 4), (1, 4), (3, 2)))
    down_weight = centred(splits[4], (EXPERTS, FF, D), FF ** -0.5, 0.15625, ((0, 4), (1, 2), (2, 4)))
    return dict(grad_out=grad_out, routes=routes, gates=gates, hidden_saved=hidden_saved, down_weight=down_weight)


def reference(grad_out, routes, gates, hidden_saved, down_weight):
    blocks = N_DP * N_EXPERT
    per_block = TOK_DEV * TOP
    pair_routes = routes.reshape(blocks, per_block).astype(jnp.int32)
    expert_ids = jnp.arange(EXPERTS, dtype=jnp.int32)
    onehot = (pair_routes[:, :, None] == expert_ids[None, None, :]).astype(jnp.int32)
    before = jnp.cumsum(onehot, axis=1) - onehot
    slot_ids = jnp.sum(before * onehot, axis=2).astype(jnp.int32)
    block_ids = jnp.broadcast_to(jnp.arange(blocks, dtype=jnp.int32)[:, None], (blocks, per_block))
    token_ids = (block_ids * TOK_DEV + jnp.arange(per_block, dtype=jnp.int32)[None, :] // TOP).astype(jnp.int32)
    row_table = jnp.zeros((blocks, EXPERTS, CAP), jnp.int32).at[block_ids, pair_routes, slot_ids].set(token_ids + 1)
    gate_table = jnp.zeros((blocks, EXPERTS, CAP), gates.dtype).at[block_ids, pair_routes, slot_ids].set(gates.reshape(blocks, per_block))
    saved = hidden_saved.reshape(N_DP, EXPERTS, N_EXPERT, CAP, FF).transpose(0, 2, 1, 3, 4).reshape(blocks, EXPERTS, CAP, FF)

    def expert_pass(operands):
        row_ids, gate_rows, saved_rows, weight = operands
        flat_ids = row_ids.reshape(-1)
        filled = flat_ids > 0
        picked = grad_out[jnp.maximum(flat_ids - 1, 0)]
        picked = jnp.where(filled[:, None], picked, jnp.zeros_like(picked))
        expert_grad = jnp.dot(picked, weight.T, preferred_element_type=jnp.float32)
        scale = gate_rows.reshape(-1, 1).astype(jnp.float32)
        hidden_rows = saved_rows.reshape(-1, FF).astype(jnp.float32)
        grad_hidden = (scale * expert_grad).astype(jnp.bfloat16)
        scaled = (scale * hidden_rows).astype(jnp.bfloat16)
        grad_weight = jnp.dot(scaled.T, picked, preferred_element_type=jnp.float32).astype(jnp.bfloat16)
        slot_dots = jnp.sum(hidden_rows * expert_grad, axis=1)
        return grad_weight, grad_hidden.reshape(blocks, CAP, FF), slot_dots.reshape(blocks, CAP)

    weight_grad, grad_hidden, slot_dots = lax.map(
        expert_pass,
        (jnp.moveaxis(row_table, 1, 0), jnp.moveaxis(gate_table, 1, 0), jnp.moveaxis(saved, 1, 0), down_weight))
    hidden_grad = grad_hidden.reshape(EXPERTS, N_DP, N_EXPERT, CAP, FF).transpose(1, 0, 2, 3, 4).reshape(N_DP, EXPERTS, N_EXPERT * CAP, FF)
    gate_grad = slot_dots[pair_routes, block_ids, slot_ids].reshape(TOKENS, TOP)
    return weight_grad, hidden_grad, gate_grad
```

```python
import jax
import jax.numpy as jnp
from jax import lax
from jax.sharding import PartitionSpec as P


def body(grad_out, routes, gates, hidden_saved, down_weight):
    token_count = grad_out.shape[0]
    top_count = routes.shape[1]
    exp_dev, ff_part, quarter = down_weight.shape
    groups = lax.axis_size("dp")
    senders = lax.axis_size("expert")
    slot_rows_all = hidden_saved.shape[2]
    capacity = slot_rows_all // senders
    experts = exp_dev * senders
    hidden_all = lax.all_gather(hidden_saved, "dp", axis=0, tiled=True)
    columns = lax.all_to_all(grad_out, "dp", split_axis=1, concat_axis=0, tiled=True)
    all_routes, all_gates = (
        lax.all_gather(routes, "dp", axis=0, tiled=True),
        lax.all_gather(gates, "dp", axis=0, tiled=True),
    )
    pair_routes = all_routes.reshape(groups, token_count * top_count)
    expert_ids = jnp.arange(experts, dtype=jnp.int32)
    onehot = (pair_routes[:, :, None] == expert_ids[None, None, :]).astype(jnp.int32)
    before = jnp.cumsum(onehot, axis=1) - onehot
    slot_ids = jnp.sum(before * onehot, axis=2)
    group_ids = jnp.arange(groups, dtype=jnp.int32)[:, None]
    position = ((group_ids * experts + pair_routes) * capacity + slot_ids).reshape(-1)
    source_rows = (
        group_ids * token_count
        + jnp.arange(token_count * top_count, dtype=jnp.int32)[None, :] // top_count
    ).reshape(-1)
    row_table = (
        jnp.zeros((groups * experts * capacity,), jnp.int32).at[position].set(source_rows + 1)
    )
    gate_table = (
        jnp.zeros((groups * experts * capacity,), gates.dtype)
        .at[position]
        .set(all_gates.reshape(-1))
    )
    row_table = (
        row_table.reshape(groups, senders, exp_dev, capacity).transpose(2, 0, 1, 3).reshape(-1)
    )
    gate_table = gate_table.reshape(groups, senders, exp_dev, capacity).transpose(2, 0, 1, 3)
    filled = row_table > 0
    safe_rows = jnp.maximum(row_table - 1, 0)
    picked = jnp.where(filled[:, None], columns[safe_rows], jnp.zeros((1, quarter), columns.dtype))
    picked = picked.reshape(exp_dev, groups, senders, capacity, quarter)
    hidden_all, picked = lax.optimization_barrier((hidden_all, picked))
    received, got_gates = (
        lax.all_to_all(picked, "expert", split_axis=2, concat_axis=2, tiled=True),
        lax.all_to_all(gate_table, "expert", split_axis=2, concat_axis=2, tiled=True),
    )
    received = received.reshape(exp_dev, groups, slot_rows_all, quarter)
    got_gates = got_gates.reshape(exp_dev, groups, slot_rows_all)
    slot_rows = received
    slot_gates = got_gates.astype(jnp.float32)
    hidden_rows = hidden_all.astype(jnp.float32)
    scaled = (jnp.moveaxis(slot_gates, 0, 1)[..., None] * hidden_rows).astype(jnp.bfloat16)
    weight_sum = jnp.einsum("nerf,enrd->efd", scaled, slot_rows, preferred_element_type=jnp.float32)
    weight_grad = weight_sum.astype(jnp.bfloat16)
    partial = jnp.einsum("enrd,efd->nerf", slot_rows, down_weight, preferred_element_type=jnp.float32)
    dot_part = jnp.sum(hidden_rows * partial, axis=3)
    me = lax.axis_index("dp")
    sent = partial.astype(jnp.bfloat16)
    expert_grad = lax.dynamic_index_in_dim(partial, me, 0, keepdims=False)
    for shift in range(1, groups):
        chunk = lax.dynamic_index_in_dim(sent, (me + shift) % groups, 0, keepdims=False)
        pairs = [(i, (i + shift) % groups) for i in range(groups)]
        expert_grad = expert_grad + lax.ppermute(chunk, "dp", pairs).astype(jnp.float32)
    own_gates = lax.dynamic_index_in_dim(got_gates, me, 1, keepdims=False).astype(jnp.float32)
    hidden_grad = (own_gates[..., None] * expert_grad).astype(jnp.bfloat16)[None]
    slot_dots = lax.psum(dot_part, ("dp", "etp"))
    slot_dots = lax.dynamic_index_in_dim(slot_dots, me, 0, keepdims=False)
    slot_dots = slot_dots.reshape(exp_dev, senders, capacity)
    returned = lax.all_to_all(slot_dots, "expert", split_axis=1, concat_axis=1, tiled=True)
    own_slots = lax.dynamic_slice_in_dim(slot_ids, lax.axis_index("dp"), 1, 0).reshape(
        token_count, top_count
    )
    lookup = (routes % exp_dev * senders + routes // exp_dev) * capacity + own_slots
    gate_grad = returned.reshape(-1)[lookup]
    return (weight_grad, hidden_grad, gate_grad)


def solution(mesh):
    in_specs = (
        P(("dp", "expert"), None),
        P(("dp", "expert"), None),
        P(("dp", "expert"), None),
        P("dp", "expert", None, "etp"),
        P("expert", "etp", "dp"),
    )
    out_specs = (
        P("expert", "etp", "dp"),
        P("dp", "expert", None, "etp"),
        P(("dp", "expert"), None),
    )
    return jax.shard_map(body, mesh=mesh, in_specs=in_specs, out_specs=out_specs, check_vma=False)
```

```python
import jax
import jax.numpy as jnp
from jax import lax
from jax.sharding import PartitionSpec as P


def body(grad_out, routes, gates, hidden_saved, down_weight):
    token_count = grad_out.shape[0]
    top_count = routes.shape[1]
    exp_dev, ff_part, quarter = down_weight.shape
    groups = lax.axis_size("dp")
    senders = lax.axis_size("expert")
    slot_rows_all = hidden_saved.shape[2]
    capacity = slot_rows_all // senders
    experts = exp_dev * senders
    meta = jnp.concatenate([routes.astype(jnp.float32), gates.astype(jnp.float32)], axis=1)
    all_meta = lax.all_gather(meta, "dp", axis=0, tiled=True)
    hidden_saved, all_meta = lax.optimization_barrier((hidden_saved, all_meta))
    hidden_all = lax.all_gather(hidden_saved, "dp", axis=0, tiled=True)
    all_routes = all_meta[:, :top_count].astype(jnp.int32)
    all_gates = all_meta[:, top_count:].astype(gates.dtype)
    columns = lax.all_to_all(grad_out, "dp", split_axis=1, concat_axis=0, tiled=True)
    pair_routes = all_routes.reshape(groups, token_count * top_count)
    expert_ids = jnp.arange(experts, dtype=jnp.int32)
    onehot = (pair_routes[:, :, None] == expert_ids[None, None, :]).astype(jnp.int32)
    before = jnp.cumsum(onehot, axis=1) - onehot
    slot_ids = jnp.sum(before * onehot, axis=2)
    group_ids = jnp.arange(groups, dtype=jnp.int32)[:, None]
    position = ((group_ids * experts + pair_routes) * capacity + slot_ids).reshape(-1)
    source_rows = (
        group_ids * token_count
        + jnp.arange(token_count * top_count, dtype=jnp.int32)[None, :] // top_count
    ).reshape(-1)
    row_table = (
        jnp.zeros((groups * experts * capacity,), jnp.int32).at[position].set(source_rows + 1)
    )
    gate_table = (
        jnp.zeros((groups * experts * capacity,), gates.dtype)
        .at[position]
        .set(all_gates.reshape(-1))
    )
    row_table = (
        row_table.reshape(groups, senders, exp_dev, capacity).transpose(2, 0, 1, 3).reshape(-1)
    )
    gate_table = gate_table.reshape(groups, senders, exp_dev, capacity).transpose(2, 0, 1, 3)
    filled = row_table > 0
    safe_rows = jnp.maximum(row_table - 1, 0)
    picked = jnp.where(filled[:, None], columns[safe_rows], jnp.zeros((1, quarter), columns.dtype))
    picked = picked.reshape(exp_dev, groups, senders, capacity, quarter)
    received, got_gates = (
        lax.all_to_all(picked, "expert", split_axis=2, concat_axis=2, tiled=True),
        lax.all_to_all(gate_table, "expert", split_axis=2, concat_axis=2, tiled=True),
    )
    received = received.reshape(exp_dev, groups, slot_rows_all, quarter)
    hidden_all, received = lax.optimization_barrier((hidden_all, received))
    got_gates = got_gates.reshape(exp_dev, groups, slot_rows_all)
    slot_rows = received
    slot_gates = got_gates.astype(jnp.float32)
    hidden_rows = hidden_all.astype(jnp.float32)
    scaled = (jnp.moveaxis(slot_gates, 0, 1)[..., None] * hidden_rows).astype(jnp.bfloat16)
    weight_sum = jnp.einsum("nerf,enrd->efd", scaled, slot_rows, preferred_element_type=jnp.float32)
    weight_grad = weight_sum.astype(jnp.bfloat16)
    partial = jnp.einsum("enrd,efd->nerf", slot_rows, down_weight, preferred_element_type=jnp.float32)
    dot_part = jnp.sum(hidden_rows * partial, axis=3)
    me = lax.axis_index("dp")
    sent = partial.astype(jnp.bfloat16)
    expert_grad = lax.dynamic_index_in_dim(partial, me, 0, keepdims=False)
    for shift in range(1, groups):
        chunk = lax.dynamic_index_in_dim(sent, (me + shift) % groups, 0, keepdims=False)
        pairs = [(i, (i + shift) % groups) for i in range(groups)]
        expert_grad = expert_grad + lax.ppermute(chunk, "dp", pairs).astype(jnp.float32)
    own_gates = lax.dynamic_index_in_dim(got_gates, me, 1, keepdims=False).astype(jnp.float32)
    hidden_grad = (own_gates[..., None] * expert_grad).astype(jnp.bfloat16)[None]
    expert_grad, dot_part, weight_grad = lax.optimization_barrier((expert_grad, dot_part, weight_grad))
    slot_dots = lax.psum(dot_part, ("dp", "etp"))
    slot_dots = lax.dynamic_index_in_dim(slot_dots, me, 0, keepdims=False)
    slot_dots = slot_dots.reshape(exp_dev, senders, capacity)
    returned = lax.all_to_all(slot_dots, "expert", split_axis=1, concat_axis=1, tiled=True)
    own_slots = lax.dynamic_slice_in_dim(slot_ids, lax.axis_index("dp"), 1, 0).reshape(
        token_count, top_count
    )
    lookup = (routes % exp_dev * senders + routes // exp_dev) * capacity + own_slots
    gate_grad = returned.reshape(-1)[lookup]
    return (weight_grad, hidden_grad, gate_grad)


def solution(mesh):
    in_specs = (
        P(("dp", "expert"), None),
        P(("dp", "expert"), None),
        P(("dp", "expert"), None),
        P("dp", "expert", None, "etp"),
        P("expert", "etp", "dp"),
    )
    out_specs = (
        P("expert", "etp", "dp"),
        P("dp", "expert", None, "etp"),
        P(("dp", "expert"), None),
    )
    return jax.shard_map(body, mesh=mesh, in_specs=in_specs, out_specs=out_specs, check_vma=False)
```

```python
import jax
import jax.numpy as jnp
from jax import lax
from jax.sharding import PartitionSpec as P


def body(grad_out, routes, gates, hidden_saved, down_weight):
    token_count = grad_out.shape[0]
    top_count = routes.shape[1]
    exp_dev, ff_part, quarter = down_weight.shape
    groups = lax.axis_size("dp")
    senders = lax.axis_size("expert")
    slot_rows_all = hidden_saved.shape[2]
    capacity = slot_rows_all // senders
    experts = exp_dev * senders
    meta = jnp.concatenate([routes.astype(jnp.float32), gates.astype(jnp.float32)], axis=1)
    all_meta = lax.all_gather(meta, "dp", axis=0, tiled=True)
    hidden_saved, all_meta = lax.optimization_barrier((hidden_saved, all_meta))
    hidden_all = lax.all_gather(hidden_saved, "dp", axis=0, tiled=True)
    all_routes = all_meta[:, :top_count].astype(jnp.int32)
    all_gates = all_meta[:, top_count:].astype(gates.dtype)
    columns = lax.all_to_all(grad_out, "dp", split_axis=1, concat_axis=0, tiled=True)
    pair_count = token_count * top_count
    pair_routes = all_routes.reshape(groups, pair_count)
    expert_ids = jnp.arange(experts, dtype=jnp.int32)
    onehot = (pair_routes[:, :, None] == expert_ids[None, None, :]).astype(jnp.bfloat16)
    pair_ids = jnp.arange(pair_count, dtype=jnp.int32)
    earlier = (pair_ids[:, None] > pair_ids[None, :]).astype(jnp.bfloat16)
    before = jnp.einsum("jk,gke->gje", earlier, onehot, preferred_element_type=jnp.float32)
    slot_ids = jnp.sum(before * onehot.astype(jnp.float32), axis=2).astype(jnp.int32)
    rows = exp_dev * senders * capacity
    position = (pair_routes % exp_dev * senders + pair_routes // exp_dev) * capacity + slot_ids
    position = position.reshape(groups, token_count, top_count)
    row_ids = jnp.arange(rows, dtype=jnp.int32)
    select = (position[..., None] == row_ids).astype(jnp.bfloat16)
    gate_rows = all_gates.reshape(groups, token_count, top_count).astype(jnp.float32)
    gate_table = jnp.einsum("gtk,gtkr->gr", gate_rows, select.astype(jnp.float32))
    token_select = jnp.sum(select, axis=2)
    picked = jnp.einsum(
        "gtr,gtd->grd",
        token_select,
        columns.reshape(groups, token_count, quarter),
        preferred_element_type=jnp.float32,
    ).astype(columns.dtype)
    picked = picked.reshape(groups, exp_dev, senders, capacity, quarter).transpose(1, 0, 2, 3, 4)
    gate_table = (
        gate_table.reshape(groups, exp_dev, senders, capacity).transpose(1, 0, 2, 3).astype(gates.dtype)
    )
    received, got_gates = (
        lax.all_to_all(picked, "expert", split_axis=2, concat_axis=2, tiled=True),
        lax.all_to_all(gate_table, "expert", split_axis=2, concat_axis=2, tiled=True),
    )
    received = received.reshape(exp_dev, groups, slot_rows_all, quarter)
    hidden_all, received = lax.optimization_barrier((hidden_all, received))
    got_gates = got_gates.reshape(exp_dev, groups, slot_rows_all)
    slot_rows = received
    slot_gates = got_gates.astype(jnp.float32)
    hidden_rows = hidden_all.astype(jnp.float32)
    scaled = (jnp.moveaxis(slot_gates, 0, 1)[..., None] * hidden_rows).astype(jnp.bfloat16)
    weight_sum = jnp.einsum("nerf,enrd->efd", scaled, slot_rows, preferred_element_type=jnp.float32)
    weight_grad = weight_sum.astype(jnp.bfloat16)
    partial = jnp.einsum("enrd,efd->nerf", slot_rows, down_weight, preferred_element_type=jnp.float32)
    dot_part = jnp.sum(hidden_rows * partial, axis=3)
    me = lax.axis_index("dp")
    sent = partial.astype(jnp.bfloat16)
    expert_grad = lax.dynamic_index_in_dim(partial, me, 0, keepdims=False)
    for shift in range(1, groups):
        chunk = lax.dynamic_index_in_dim(sent, (me + shift) % groups, 0, keepdims=False)
        pairs = [(i, (i + shift) % groups) for i in range(groups)]
        expert_grad = expert_grad + lax.ppermute(chunk, "dp", pairs).astype(jnp.float32)
    own_gates = lax.dynamic_index_in_dim(got_gates, me, 1, keepdims=False).astype(jnp.float32)
    hidden_grad = (own_gates[..., None] * expert_grad).astype(jnp.bfloat16)[None]
    expert_grad, dot_part, weight_grad = lax.optimization_barrier((expert_grad, dot_part, weight_grad))
    slot_dots = lax.psum(dot_part, ("dp", "etp"))
    slot_dots = lax.dynamic_index_in_dim(slot_dots, me, 0, keepdims=False)
    slot_dots = slot_dots.reshape(exp_dev, senders, capacity)
    returned = lax.all_to_all(slot_dots, "expert", split_axis=1, concat_axis=1, tiled=True)
    own_select = lax.dynamic_index_in_dim(select, me, 0, keepdims=False).astype(jnp.float32)
    gate_grad = jnp.sum(own_select * returned.reshape(1, 1, rows), axis=2)
    return (weight_grad, hidden_grad, gate_grad)


def solution(mesh):
    in_specs = (
        P(("dp", "expert"), None),
        P(("dp", "expert"), None),
        P(("dp", "expert"), None),
        P("dp", "expert", None, "etp"),
        P("expert", "etp", "dp"),
    )
    out_specs = (
        P("expert", "etp", "dp"),
        P("dp", "expert", None, "etp"),
        P(("dp", "expert"), None),
    )
    return jax.shard_map(body, mesh=mesh, in_specs=in_specs, out_specs=out_specs, check_vma=False)
```

```python
import jax
import jax.numpy as jnp
from jax import lax
from jax.sharding import PartitionSpec as P


def body(grad_out, routes, gates, hidden_saved, down_weight):
    token_count = grad_out.shape[0]
    top_count = routes.shape[1]
    exp_dev, ff_part, quarter = down_weight.shape
    groups = lax.axis_size("dp")
    senders = lax.axis_size("expert")
    slot_rows_all = hidden_saved.shape[2]
    capacity = slot_rows_all // senders
    experts = exp_dev * senders
    meta = jnp.concatenate([routes.astype(jnp.float32), gates.astype(jnp.float32)], axis=1)
    all_meta = lax.all_gather(meta, "dp", axis=0, tiled=True)
    columns = lax.all_to_all(grad_out, "dp", split_axis=1, concat_axis=0, tiled=True)
    hidden_saved, all_meta, columns = lax.optimization_barrier((hidden_saved, all_meta, columns))
    hidden_all = lax.all_gather(hidden_saved, "dp", axis=0, tiled=True)
    all_routes = all_meta[:, :top_count].astype(jnp.int32)
    all_gates = all_meta[:, top_count:].astype(gates.dtype)
    pair_count = token_count * top_count
    pair_routes = all_routes.reshape(groups, pair_count)
    expert_ids = jnp.arange(experts, dtype=jnp.int32)
    onehot = (pair_routes[:, :, None] == expert_ids[None, None, :]).astype(jnp.bfloat16)
    pair_ids = jnp.arange(pair_count, dtype=jnp.int32)
    earlier = (pair_ids[:, None] > pair_ids[None, :]).astype(jnp.bfloat16)
    before = jnp.einsum("jk,gke->gje", earlier, onehot, preferred_element_type=jnp.float32)
    slot_ids = jnp.sum(before * onehot.astype(jnp.float32), axis=2).astype(jnp.int32)
    rows = exp_dev * senders * capacity
    position = (pair_routes % exp_dev * senders + pair_routes // exp_dev) * capacity + slot_ids
    position = position.reshape(groups, token_count, top_count)
    row_ids = jnp.arange(rows, dtype=jnp.int32)
    select = (position[..., None] == row_ids).astype(jnp.bfloat16)
    gate_rows = all_gates.reshape(groups, token_count, top_count).astype(jnp.float32)
    gate_table = jnp.einsum("gtk,gtkr->gr", gate_rows, select.astype(jnp.float32))
    token_select = jnp.sum(select, axis=2)
    picked = jnp.einsum(
        "gtr,gtd->grd",
        token_select,
        columns.reshape(groups, token_count, quarter),
        preferred_element_type=jnp.float32,
    ).astype(columns.dtype)
    picked = picked.reshape(groups, exp_dev, senders, capacity, quarter).transpose(1, 0, 2, 3, 4)
    gate_table = (
        gate_table.reshape(groups, exp_dev, senders, capacity).transpose(1, 0, 2, 3).astype(gates.dtype)
    )
    got_gates = lax.all_to_all(gate_table, "expert", split_axis=2, concat_axis=2, tiled=True)
    got_gates = got_gates.reshape(exp_dev, groups, slot_rows_all)
    slot_gates = got_gates.astype(jnp.float32)
    me = lax.axis_index("dp")
    own_gates = lax.dynamic_index_in_dim(got_gates, me, 1, keepdims=False).astype(jnp.float32)
    chunks = 2 if exp_dev % 2 == 0 else 1
    per = exp_dev // chunks
    grads, dots, hidden_parts = [], [], []
    for c in range(chunks):
        local = slice(c * per, (c + 1) * per)
        received = lax.all_to_all(picked[local], "expert", split_axis=2, concat_axis=2, tiled=True)
        received = received.reshape(per, groups, slot_rows_all, quarter)
        if c == chunks - 1:
            hidden_all, received = lax.optimization_barrier((hidden_all, received))
        partial = jnp.einsum(
            "enrd,efd->nerf", received, down_weight[local], preferred_element_type=jnp.float32
        )
        sent = partial.astype(jnp.bfloat16)
        expert_grad = lax.dynamic_index_in_dim(partial, me, 0, keepdims=False)
        for shift in range(1, groups):
            chunk = lax.dynamic_index_in_dim(sent, (me + shift) % groups, 0, keepdims=False)
            pairs = [(i, (i + shift) % groups) for i in range(groups)]
            expert_grad = expert_grad + lax.ppermute(chunk, "dp", pairs).astype(jnp.float32)
        hidden_rows = hidden_all[:, local].astype(jnp.float32)
        dots.append(jnp.sum(hidden_rows * partial, axis=3))
        scaled = (jnp.moveaxis(slot_gates[local], 0, 1)[..., None] * hidden_rows).astype(jnp.bfloat16)
        weight_sum = jnp.einsum("nerf,enrd->efd", scaled, received, preferred_element_type=jnp.float32)
        grads.append(weight_sum.astype(jnp.bfloat16))
        hidden_parts.append((own_gates[local][..., None] * expert_grad).astype(jnp.bfloat16))
    weight_grad = jnp.concatenate(grads, axis=0)
    dot_part = jnp.concatenate(dots, axis=1)
    hidden_grad = jnp.concatenate(hidden_parts, axis=0)[None]
    hidden_grad, dot_part, weight_grad = lax.optimization_barrier((hidden_grad, dot_part, weight_grad))
    slot_dots = lax.psum(dot_part, ("dp", "etp"))
    slot_dots = lax.dynamic_index_in_dim(slot_dots, me, 0, keepdims=False)
    slot_dots = slot_dots.reshape(exp_dev, senders, capacity)
    returned = lax.all_to_all(slot_dots, "expert", split_axis=1, concat_axis=1, tiled=True)
    own_select = lax.dynamic_index_in_dim(select, me, 0, keepdims=False).astype(jnp.float32)
    gate_grad = jnp.sum(own_select * returned.reshape(1, 1, rows), axis=2)
    return (weight_grad, hidden_grad, gate_grad)


def solution(mesh):
    in_specs = (
        P(("dp", "expert"), None),
        P(("dp", "expert"), None),
        P(("dp", "expert"), None),
        P("dp", "expert", None, "etp"),
        P("expert", "etp", "dp"),
    )
    out_specs = (
        P("expert", "etp", "dp"),
        P("dp", "expert", None, "etp"),
        P(("dp", "expert"), None),
    )
    return jax.shard_map(body, mesh=mesh, in_specs=in_specs, out_specs=out_specs, check_vma=False)
```

```python
import jax
import jax.numpy as jnp
from jax import lax
from jax.sharding import PartitionSpec as P


def body(grad_out, routes, gates, hidden_saved, down_weight):
    token_count = grad_out.shape[0]
    top_count = routes.shape[1]
    exp_dev, ff_part, quarter = down_weight.shape
    groups = lax.axis_size("dp")
    senders = lax.axis_size("expert")
    slot_rows_all = hidden_saved.shape[2]
    capacity = slot_rows_all // senders
    experts = exp_dev * senders
    meta = jnp.concatenate([routes.astype(jnp.float32), gates.astype(jnp.float32)], axis=1)
    all_meta = lax.all_gather(meta, "dp", axis=0, tiled=True)
    columns = lax.all_to_all(grad_out, "dp", split_axis=1, concat_axis=0, tiled=True)
    hidden_saved, all_meta, columns = lax.optimization_barrier((hidden_saved, all_meta, columns))
    hidden_all = lax.all_gather(hidden_saved, "dp", axis=0, tiled=True)
    all_routes = all_meta[:, :top_count].astype(jnp.int32)
    all_gates = all_meta[:, top_count:].astype(gates.dtype)
    pair_count = token_count * top_count
    pair_routes = all_routes.reshape(groups, pair_count)
    expert_ids = jnp.arange(experts, dtype=jnp.int32)
    onehot = (pair_routes[:, :, None] == expert_ids[None, None, :]).astype(jnp.bfloat16)
    pair_ids = jnp.arange(pair_count, dtype=jnp.int32)
    earlier = (pair_ids[:, None] > pair_ids[None, :]).astype(jnp.bfloat16)
    before = jnp.einsum("jk,gke->gje", earlier, onehot, preferred_element_type=jnp.float32)
    slot_ids = jnp.sum(before * onehot.astype(jnp.float32), axis=2).astype(jnp.int32)
    rows = exp_dev * senders * capacity
    position = (pair_routes % exp_dev * senders + pair_routes // exp_dev) * capacity + slot_ids
    position = position.reshape(groups, token_count, top_count)
    row_ids = jnp.arange(rows, dtype=jnp.int32)
    select = (position[..., None] == row_ids).astype(jnp.bfloat16)
    gate_rows = all_gates.reshape(groups, token_count, top_count).astype(jnp.float32)
    gate_table = jnp.einsum("gtk,gtkr->gr", gate_rows, select.astype(jnp.float32))
    token_select = jnp.sum(select, axis=2)
    picked = jnp.einsum(
        "gtr,gtd->grd",
        token_select,
        columns.reshape(groups, token_count, quarter),
        preferred_element_type=jnp.float32,
    ).astype(columns.dtype)
    picked = picked.reshape(groups, exp_dev, senders, capacity, quarter).transpose(1, 0, 2, 3, 4)
    gate_table = (
        gate_table.reshape(groups, exp_dev, senders, capacity).transpose(1, 0, 2, 3).astype(gates.dtype)
    )
    got_gates = lax.all_to_all(gate_table, "expert", split_axis=2, concat_axis=2, tiled=True)
    got_gates = got_gates.reshape(exp_dev, groups, slot_rows_all)
    slot_gates = got_gates.astype(jnp.float32)
    me = lax.axis_index("dp")
    own_gates = lax.dynamic_index_in_dim(got_gates, me, 1, keepdims=False).astype(jnp.float32)
    chunks = 2 if exp_dev % 2 == 0 else 1
    per = exp_dev // chunks
    grads, dots, hidden_parts = [], [], []
    for c in range(chunks):
        local = slice(c * per, (c + 1) * per)
        received = lax.all_to_all(picked[local], "expert", split_axis=2, concat_axis=2, tiled=True)
        received = received.reshape(per, groups, slot_rows_all, quarter)
        if c == chunks - 1:
            hidden_all, received = lax.optimization_barrier((hidden_all, received))
        partial = jnp.einsum(
            "enrd,efd->nerf", received, down_weight[local], preferred_element_type=jnp.float32
        )
        sent = partial.astype(jnp.bfloat16)
        expert_grad = lax.dynamic_index_in_dim(partial, me, 0, keepdims=False)
        for shift in range(1, groups):
            chunk = lax.dynamic_index_in_dim(sent, (me + shift) % groups, 0, keepdims=False)
            pairs = [(i, (i + shift) % groups) for i in range(groups)]
            expert_grad = expert_grad + lax.ppermute(chunk, "dp", pairs).astype(jnp.float32)
        hidden_rows = hidden_all[:, local].astype(jnp.float32)
        dots.append(jnp.sum(hidden_rows * partial, axis=3))
        scaled = (jnp.moveaxis(slot_gates[local], 0, 1)[..., None] * hidden_rows).astype(jnp.bfloat16)
        weight_sum = jnp.einsum("nerf,enrd->efd", scaled, received, preferred_element_type=jnp.float32)
        grads.append(weight_sum.astype(jnp.bfloat16))
        hidden_parts.append((own_gates[local][..., None] * expert_grad).astype(jnp.bfloat16))
    weight_grad = jnp.concatenate(grads, axis=0)
    dot_part = jnp.concatenate(dots, axis=1)
    hidden_grad = jnp.concatenate(hidden_parts, axis=0)[None]
    own_dots = lax.dynamic_index_in_dim(dot_part, me, 0, keepdims=False)
    for shift in range(1, groups):
        chunk = lax.dynamic_index_in_dim(dot_part, (me + shift) % groups, 0, keepdims=False)
        pairs = [(i, (i + shift) % groups) for i in range(groups)]
        own_dots = own_dots + lax.ppermute(chunk, "dp", pairs)
    halves = lax.axis_size("etp")
    half_dots = own_dots
    for shift in range(1, halves):
        pairs = [(i, (i + shift) % halves) for i in range(halves)]
        own_dots = own_dots + lax.ppermute(half_dots, "etp", pairs)
    hidden_grad, own_dots, weight_grad = lax.optimization_barrier((hidden_grad, own_dots, weight_grad))
    slot_dots = own_dots.reshape(exp_dev, senders, capacity)
    returned = lax.all_to_all(slot_dots, "expert", split_axis=1, concat_axis=1, tiled=True)
    own_select = lax.dynamic_index_in_dim(select, me, 0, keepdims=False).astype(jnp.float32)
    gate_grad = jnp.sum(own_select * returned.reshape(1, 1, rows), axis=2)
    return (weight_grad, hidden_grad, gate_grad)


def solution(mesh):
    in_specs = (
        P(("dp", "expert"), None),
        P(("dp", "expert"), None),
        P(("dp", "expert"), None),
        P("dp", "expert", None, "etp"),
        P("expert", "etp", "dp"),
    )
    out_specs = (
        P("expert", "etp", "dp"),
        P("dp", "expert", None, "etp"),
        P(("dp", "expert"), None),
    )
    return jax.shard_map(body, mesh=mesh, in_specs=in_specs, out_specs=out_specs, check_vma=False)
```

```python
import jax
import jax.numpy as jnp
from jax import lax
from jax.sharding import PartitionSpec as P


def line_sum(partial, me, n):
    right = left = None
    for step in range(1, n):
        target = jnp.clip(me + n - step, 0, n - 1)
        ahead = lax.dynamic_index_in_dim(partial, target, 0, keepdims=False)
        if right is not None:
            ahead = ahead + right.astype(jnp.float32)
        right = lax.ppermute(ahead.astype(jnp.bfloat16), "dp", [(i, i + 1) for i in range(step)])
        target = jnp.clip(me - n + step, 0, n - 1)
        behind = lax.dynamic_index_in_dim(partial, target, 0, keepdims=False)
        if left is not None:
            behind = behind + left.astype(jnp.float32)
        left = lax.ppermute(behind.astype(jnp.bfloat16), "dp", [(i, i - 1) for i in range(n - step, n)])
    own = lax.dynamic_index_in_dim(partial, me, 0, keepdims=False)
    return own + right.astype(jnp.float32) + left.astype(jnp.float32)


def body(grad_out, routes, gates, hidden_saved, down_weight):
    token_count = grad_out.shape[0]
    top_count = routes.shape[1]
    exp_dev, ff_part, quarter = down_weight.shape
    groups = lax.axis_size("dp")
    senders = lax.axis_size("expert")
    slot_rows_all = hidden_saved.shape[2]
    capacity = slot_rows_all // senders
    experts = exp_dev * senders
    meta = jnp.concatenate([routes.astype(jnp.float32), gates.astype(jnp.float32)], axis=1)
    all_meta = lax.all_gather(meta, "dp", axis=0, tiled=True)
    columns = lax.all_to_all(grad_out, "dp", split_axis=1, concat_axis=0, tiled=True)
    hidden_saved, all_meta, columns = lax.optimization_barrier((hidden_saved, all_meta, columns))
    hidden_all = lax.all_gather(hidden_saved, "dp", axis=0, tiled=True)
    all_routes = all_meta[:, :top_count].astype(jnp.int32)
    all_gates = all_meta[:, top_count:].astype(gates.dtype)
    pair_count = token_count * top_count
    pair_routes = all_routes.reshape(groups, pair_count)
    expert_ids = jnp.arange(experts, dtype=jnp.int32)
    onehot = (pair_routes[:, :, None] == expert_ids[None, None, :]).astype(jnp.bfloat16)
    pair_ids = jnp.arange(pair_count, dtype=jnp.int32)
    earlier = (pair_ids[:, None] > pair_ids[None, :]).astype(jnp.bfloat16)
    before = jnp.einsum("jk,gke->gje", earlier, onehot, preferred_element_type=jnp.float32)
    slot_ids = jnp.sum(before * onehot.astype(jnp.float32), axis=2).astype(jnp.int32)
    rows = exp_dev * senders * capacity
    position = (pair_routes % exp_dev * senders + pair_routes // exp_dev) * capacity + slot_ids
    position = position.reshape(groups, token_count, top_count)
    row_ids = jnp.arange(rows, dtype=jnp.int32)
    select = (position[..., None] == row_ids).astype(jnp.bfloat16)
    gate_rows = all_gates.reshape(groups, token_count, top_count).astype(jnp.float32)
    gate_table = jnp.einsum("gtk,gtkr->gr", gate_rows, select.astype(jnp.float32))
    token_select = jnp.sum(select, axis=2)
    picked = jnp.einsum(
        "gtr,gtd->grd",
        token_select,
        columns.reshape(groups, token_count, quarter),
        preferred_element_type=jnp.float32,
    ).astype(columns.dtype)
    picked = picked.reshape(groups, exp_dev, senders, capacity, quarter).transpose(1, 0, 2, 3, 4)
    gate_table = (
        gate_table.reshape(groups, exp_dev, senders, capacity).transpose(1, 0, 2, 3).astype(gates.dtype)
    )
    got_gates = lax.all_to_all(gate_table, "expert", split_axis=2, concat_axis=2, tiled=True)
    got_gates = got_gates.reshape(exp_dev, groups, slot_rows_all)
    slot_gates = got_gates.astype(jnp.float32)
    me = lax.axis_index("dp")
    own_gates = lax.dynamic_index_in_dim(got_gates, me, 1, keepdims=False).astype(jnp.float32)
    chunks = 2 if exp_dev % 2 == 0 else 1
    per = exp_dev // chunks
    grads, dots, hidden_parts = [], [], []
    for c in range(chunks):
        local = slice(c * per, (c + 1) * per)
        received = lax.all_to_all(picked[local], "expert", split_axis=2, concat_axis=2, tiled=True)
        received = received.reshape(per, groups, slot_rows_all, quarter)
        if c == chunks - 1:
            hidden_all, received = lax.optimization_barrier((hidden_all, received))
        partial = jnp.einsum(
            "enrd,efd->nerf", received, down_weight[local], preferred_element_type=jnp.float32
        )
        expert_grad = line_sum(partial, me, groups)
        hidden_rows = hidden_all[:, local].astype(jnp.float32)
        dots.append(jnp.sum(hidden_rows * partial, axis=3))
        scaled = (jnp.moveaxis(slot_gates[local], 0, 1)[..., None] * hidden_rows).astype(jnp.bfloat16)
        weight_sum = jnp.einsum("nerf,enrd->efd", scaled, received, preferred_element_type=jnp.float32)
        grads.append(weight_sum.astype(jnp.bfloat16))
        hidden_parts.append((own_gates[local][..., None] * expert_grad).astype(jnp.bfloat16))
    weight_grad = jnp.concatenate(grads, axis=0)
    dot_part = jnp.concatenate(dots, axis=1)
    hidden_grad = jnp.concatenate(hidden_parts, axis=0)[None]
    own_dots = lax.dynamic_index_in_dim(dot_part, me, 0, keepdims=False)
    for shift in range(1, groups):
        chunk = lax.dynamic_index_in_dim(dot_part, (me + shift) % groups, 0, keepdims=False)
        pairs = [(i, (i + shift) % groups) for i in range(groups)]
        own_dots = own_dots + lax.ppermute(chunk, "dp", pairs)
    halves = lax.axis_size("etp")
    half_dots = own_dots
    for shift in range(1, halves):
        pairs = [(i, (i + shift) % halves) for i in range(halves)]
        own_dots = own_dots + lax.ppermute(half_dots, "etp", pairs)
    hidden_grad, own_dots, weight_grad = lax.optimization_barrier((hidden_grad, own_dots, weight_grad))
    slot_dots = own_dots.reshape(exp_dev, senders, capacity)
    returned = lax.all_to_all(slot_dots, "expert", split_axis=1, concat_axis=1, tiled=True)
    own_select = lax.dynamic_index_in_dim(select, me, 0, keepdims=False).astype(jnp.float32)
    gate_grad = jnp.sum(own_select * returned.reshape(1, 1, rows), axis=2)
    return (weight_grad, hidden_grad, gate_grad)


def solution(mesh):
    in_specs = (
        P(("dp", "expert"), None),
        P(("dp", "expert"), None),
        P(("dp", "expert"), None),
        P("dp", "expert", None, "etp"),
        P("expert", "etp", "dp"),
    )
    out_specs = (
        P("expert", "etp", "dp"),
        P("dp", "expert", None, "etp"),
        P(("dp", "expert"), None),
    )
    return jax.shard_map(body, mesh=mesh, in_specs=in_specs, out_specs=out_specs, check_vma=False)
```

```python
import jax
import jax.numpy as jnp
from jax import lax
from jax.sharding import PartitionSpec as P


def body(grad_out, routes, gates, hidden_saved, down_weight):
    token_count = grad_out.shape[0]
    top_count = routes.shape[1]
    exp_dev, ff_part, quarter = down_weight.shape
    groups = lax.axis_size("dp")
    senders = lax.axis_size("expert")
    slot_rows_all = hidden_saved.shape[2]
    capacity = slot_rows_all // senders
    experts = exp_dev * senders
    meta = jnp.concatenate([routes.astype(jnp.float32), gates.astype(jnp.float32)], axis=1)
    all_meta = lax.all_gather(meta, "dp", axis=0, tiled=True)
    columns = lax.all_to_all(grad_out, "dp", split_axis=1, concat_axis=0, tiled=True)
    hidden_saved, all_meta, columns = lax.optimization_barrier((hidden_saved, all_meta, columns))
    hidden_all = lax.all_gather(hidden_saved, "dp", axis=0, tiled=True)
    all_routes = all_meta[:, :top_count].astype(jnp.int32)
    all_gates = all_meta[:, top_count:].astype(gates.dtype)
    pair_count = token_count * top_count
    pair_routes = all_routes.reshape(groups, pair_count)
    expert_ids = jnp.arange(experts, dtype=jnp.int32)
    onehot = (pair_routes[:, :, None] == expert_ids[None, None, :]).astype(jnp.bfloat16)
    pair_ids = jnp.arange(pair_count, dtype=jnp.int32)
    earlier = (pair_ids[:, None] > pair_ids[None, :]).astype(jnp.bfloat16)
    before = jnp.einsum("jk,gke->gje", earlier, onehot, preferred_element_type=jnp.float32)
    slot_ids = jnp.sum(before * onehot.astype(jnp.float32), axis=2).astype(jnp.int32)
    rows = exp_dev * senders * capacity
    position = (pair_routes % exp_dev * senders + pair_routes // exp_dev) * capacity + slot_ids
    position = position.reshape(groups, token_count, top_count)
    row_ids = jnp.arange(rows, dtype=jnp.int32)
    select = (position[..., None] == row_ids).astype(jnp.bfloat16)
    gate_rows = all_gates.reshape(groups, token_count, top_count).astype(jnp.float32)
    gate_table = jnp.einsum("gtk,gtkr->gr", gate_rows, select.astype(jnp.float32))
    token_select = jnp.sum(select, axis=2)
    token_select = token_select.reshape(groups, token_count, exp_dev, senders, capacity)
    token_columns = columns.reshape(groups, token_count, quarter)
    gate_table = (
        gate_table.reshape(groups, exp_dev, senders, capacity).transpose(1, 0, 2, 3).astype(gates.dtype)
    )
    got_gates = lax.all_to_all(gate_table, "expert", split_axis=2, concat_axis=2, tiled=True)
    got_gates = got_gates.reshape(exp_dev, groups, slot_rows_all)
    slot_gates = got_gates.astype(jnp.float32)
    me = lax.axis_index("dp")
    own_gates = lax.dynamic_index_in_dim(got_gates, me, 1, keepdims=False).astype(jnp.float32)
    chunks = 2 if exp_dev % 2 == 0 else 1
    per = exp_dev // chunks
    grads, dots, hidden_parts = [], [], []
    for c in range(chunks):
        local = slice(c * per, (c + 1) * per)
        picked = jnp.einsum(
            "gtlqs,gtd->qglsd",
            token_select[:, :, local],
            token_columns,
            preferred_element_type=jnp.float32,
        ).astype(columns.dtype)
        received = lax.all_to_all(picked, "expert", split_axis=0, concat_axis=0, tiled=True)
        if c == chunks - 1:
            hidden_all, received = lax.optimization_barrier((hidden_all, received))
        partial = jnp.einsum(
            "qglsd,lfd->glqsf", received, down_weight[local], preferred_element_type=jnp.float32
        ).reshape(groups, per, slot_rows_all, ff_part)
        sent = partial.astype(jnp.bfloat16)
        expert_grad = lax.dynamic_index_in_dim(partial, me, 0, keepdims=False)
        for shift in range(1, groups):
            chunk = lax.dynamic_index_in_dim(sent, (me + shift) % groups, 0, keepdims=False)
            pairs = [(i, (i + shift) % groups) for i in range(groups)]
            expert_grad = expert_grad + lax.ppermute(chunk, "dp", pairs).astype(jnp.float32)
        hidden_rows = hidden_all[:, local].astype(jnp.float32)
        dots.append(jnp.sum(hidden_rows * partial, axis=3))
        scaled = (jnp.moveaxis(slot_gates[local], 0, 1)[..., None] * hidden_rows).astype(jnp.bfloat16)
        scaled = scaled.reshape(groups, per, senders, capacity, ff_part)
        weight_sum = jnp.einsum("glqsf,qglsd->lfd", scaled, received, preferred_element_type=jnp.float32)
        grads.append(weight_sum.astype(jnp.bfloat16))
        hidden_parts.append((own_gates[local][..., None] * expert_grad).astype(jnp.bfloat16))
    weight_grad = jnp.concatenate(grads, axis=0)
    dot_part = jnp.concatenate(dots, axis=1)
    hidden_grad = jnp.concatenate(hidden_parts, axis=0)[None]
    own_dots = lax.dynamic_index_in_dim(dot_part, me, 0, keepdims=False)
    for shift in range(1, groups):
        chunk = lax.dynamic_index_in_dim(dot_part, (me + shift) % groups, 0, keepdims=False)
        pairs = [(i, (i + shift) % groups) for i in range(groups)]
        own_dots = own_dots + lax.ppermute(chunk, "dp", pairs)
    halves = lax.axis_size("etp")
    half_dots = own_dots
    for shift in range(1, halves):
        pairs = [(i, (i + shift) % halves) for i in range(halves)]
        own_dots = own_dots + lax.ppermute(half_dots, "etp", pairs)
    hidden_grad, own_dots, weight_grad = lax.optimization_barrier((hidden_grad, own_dots, weight_grad))
    slot_dots = own_dots.reshape(exp_dev, senders, capacity)
    returned = lax.all_to_all(slot_dots, "expert", split_axis=1, concat_axis=1, tiled=True)
    own_select = lax.dynamic_index_in_dim(select, me, 0, keepdims=False).astype(jnp.float32)
    gate_grad = jnp.sum(own_select * returned.reshape(1, 1, rows), axis=2)
    return (weight_grad, hidden_grad, gate_grad)


def solution(mesh):
    in_specs = (
        P(("dp", "expert"), None),
        P(("dp", "expert"), None),
        P(("dp", "expert"), None),
        P("dp", "expert", None, "etp"),
        P("expert", "etp", "dp"),
    )
    out_specs = (
        P("expert", "etp", "dp"),
        P("dp", "expert", None, "etp"),
        P(("dp", "expert"), None),
    )
    return jax.shard_map(body, mesh=mesh, in_specs=in_specs, out_specs=out_specs, check_vma=False)
```

```python
import jax
import jax.numpy as jnp
from jax import lax
from jax.sharding import PartitionSpec as P


def body(grad_out, routes, gates, hidden_saved, down_weight):
    token_count = grad_out.shape[0]
    top_count = routes.shape[1]
    exp_dev, ff_part, quarter = down_weight.shape
    groups = lax.axis_size("dp")
    senders = lax.axis_size("expert")
    slot_rows_all = hidden_saved.shape[2]
    capacity = slot_rows_all // senders
    experts = exp_dev * senders
    meta = jnp.concatenate([routes.astype(jnp.float32), gates.astype(jnp.float32)], axis=1)
    all_meta = lax.all_gather(meta, "dp", axis=0, tiled=True)
    columns = lax.all_to_all(grad_out, "dp", split_axis=1, concat_axis=0, tiled=True)
    hidden_saved, all_meta, columns = lax.optimization_barrier((hidden_saved, all_meta, columns))
    hidden_all = lax.all_gather(hidden_saved, "dp", axis=0, tiled=True)
    all_routes = all_meta[:, :top_count].astype(jnp.int32)
    all_gates = all_meta[:, top_count:].astype(gates.dtype)
    pair_count = token_count * top_count
    pair_routes = all_routes.reshape(groups, pair_count)
    expert_ids = jnp.arange(experts, dtype=jnp.int32)
    onehot = (pair_routes[:, :, None] == expert_ids[None, None, :]).astype(jnp.bfloat16)
    pair_ids = jnp.arange(pair_count, dtype=jnp.int32)
    earlier = (pair_ids[:, None] > pair_ids[None, :]).astype(jnp.bfloat16)
    before = jnp.einsum("jk,gke->gje", earlier, onehot, preferred_element_type=jnp.float32)
    slot_ids = jnp.sum(before * onehot.astype(jnp.float32), axis=2).astype(jnp.int32)
    rows = exp_dev * senders * capacity
    position = (pair_routes % exp_dev * senders + pair_routes // exp_dev) * capacity + slot_ids
    position = position.reshape(groups, token_count, top_count)
    row_ids = jnp.arange(rows, dtype=jnp.int32)
    select = (position[..., None] == row_ids).astype(jnp.bfloat16)
    gate_rows = all_gates.reshape(groups, token_count, top_count).astype(jnp.float32)
    gate_table = jnp.einsum("gtk,gtkr->gr", gate_rows, select.astype(jnp.float32))
    token_select = jnp.sum(select, axis=2)
    token_select = token_select.reshape(groups, token_count, exp_dev, senders, capacity)
    token_columns = columns.reshape(groups, token_count, quarter)
    gate_table = (
        gate_table.reshape(groups, exp_dev, senders, capacity).transpose(1, 0, 2, 3).astype(gates.dtype)
    )
    got_gates = lax.all_to_all(gate_table, "expert", split_axis=2, concat_axis=2, tiled=True)
    got_gates = got_gates.reshape(exp_dev, groups, slot_rows_all)
    slot_gates = got_gates.astype(jnp.float32)
    me = lax.axis_index("dp")
    own_gates = lax.dynamic_index_in_dim(got_gates, me, 1, keepdims=False).astype(jnp.float32)
    chunks = 2 if exp_dev % 2 == 0 else 1
    per = exp_dev // chunks
    grads, dots, hidden_parts = [], [], []
    for c in range(chunks):
        local = slice(c * per, (c + 1) * per)
        picked = jnp.einsum(
            "gtlqs,gtd->qglsd",
            token_select[:, :, local],
            token_columns,
            preferred_element_type=jnp.float32,
        ).astype(columns.dtype)
        received = lax.all_to_all(picked, "expert", split_axis=0, concat_axis=0, tiled=True)
        if c == chunks - 1:
            hidden_all, received = lax.optimization_barrier((hidden_all, received))
        partial = jnp.einsum(
            "qglsd,lfd->glqsf", received, down_weight[local], preferred_element_type=jnp.float32
        ).reshape(groups, per, slot_rows_all, ff_part)
        arrived = lax.all_to_all(partial.astype(jnp.bfloat16), "dp", split_axis=0, concat_axis=0, tiled=True)
        expert_grad = jnp.sum(arrived.astype(jnp.float32), axis=0)
        hidden_rows = hidden_all[:, local].astype(jnp.float32)
        dots.append(jnp.sum(hidden_rows * partial, axis=3))
        scaled = (jnp.moveaxis(slot_gates[local], 0, 1)[..., None] * hidden_rows).astype(jnp.bfloat16)
        scaled = scaled.reshape(groups, per, senders, capacity, ff_part)
        weight_sum = jnp.einsum("glqsf,qglsd->lfd", scaled, received, preferred_element_type=jnp.float32)
        grads.append(weight_sum.astype(jnp.bfloat16))
        hidden_parts.append((own_gates[local][..., None] * expert_grad).astype(jnp.bfloat16))
    weight_grad = jnp.concatenate(grads, axis=0)
    dot_part = jnp.concatenate(dots, axis=1)
    hidden_grad = jnp.concatenate(hidden_parts, axis=0)[None]
    own_dots = lax.dynamic_index_in_dim(dot_part, me, 0, keepdims=False)
    for shift in range(1, groups):
        chunk = lax.dynamic_index_in_dim(dot_part, (me + shift) % groups, 0, keepdims=False)
        pairs = [(i, (i + shift) % groups) for i in range(groups)]
        own_dots = own_dots + lax.ppermute(chunk, "dp", pairs)
    halves = lax.axis_size("etp")
    half_dots = own_dots
    for shift in range(1, halves):
        pairs = [(i, (i + shift) % halves) for i in range(halves)]
        own_dots = own_dots + lax.ppermute(half_dots, "etp", pairs)
    hidden_grad, own_dots, weight_grad = lax.optimization_barrier((hidden_grad, own_dots, weight_grad))
    slot_dots = own_dots.reshape(exp_dev, senders, capacity)
    returned = lax.all_to_all(slot_dots, "expert", split_axis=1, concat_axis=1, tiled=True)
    own_select = lax.dynamic_index_in_dim(select, me, 0, keepdims=False).astype(jnp.float32)
    gate_grad = jnp.sum(own_select * returned.reshape(1, 1, rows), axis=2)
    return (weight_grad, hidden_grad, gate_grad)


def solution(mesh):
    in_specs = (
        P(("dp", "expert"), None),
        P(("dp", "expert"), None),
        P(("dp", "expert"), None),
        P("dp", "expert", None, "etp"),
        P("expert", "etp", "dp"),
    )
    out_specs = (
        P("expert", "etp", "dp"),
        P("dp", "expert", None, "etp"),
        P(("dp", "expert"), None),
    )
    return jax.shard_map(body, mesh=mesh, in_specs=in_specs, out_specs=out_specs, check_vma=False)
```

```python
import jax
import jax.numpy as jnp
from jax import lax
from jax.sharding import PartitionSpec as P


def body(grad_out, routes, gates, hidden_saved, down_weight):
    token_count = grad_out.shape[0]
    top_count = routes.shape[1]
    exp_dev, ff_part, quarter = down_weight.shape
    groups = lax.axis_size("dp")
    senders = lax.axis_size("expert")
    slot_rows_all = hidden_saved.shape[2]
    capacity = slot_rows_all // senders
    experts = exp_dev * senders
    meta = jnp.concatenate([routes.astype(jnp.float32), gates.astype(jnp.float32)], axis=1)
    all_meta = lax.all_gather(meta, "dp", axis=0, tiled=True)
    columns = lax.all_to_all(grad_out, "dp", split_axis=1, concat_axis=0, tiled=True)
    hidden_saved, all_meta, columns = lax.optimization_barrier((hidden_saved, all_meta, columns))
    hidden_all = lax.all_gather(hidden_saved, "dp", axis=0, tiled=True)
    all_routes = all_meta[:, :top_count].astype(jnp.int32)
    all_gates = all_meta[:, top_count:].astype(gates.dtype)
    pair_count = token_count * top_count
    pair_routes = all_routes.reshape(groups, pair_count)
    expert_ids = jnp.arange(experts, dtype=jnp.int32)
    onehot = (pair_routes[:, :, None] == expert_ids[None, None, :]).astype(jnp.bfloat16)
    pair_ids = jnp.arange(pair_count, dtype=jnp.int32)
    earlier = (pair_ids[:, None] > pair_ids[None, :]).astype(jnp.bfloat16)
    before = jnp.einsum("jk,gke->gje", earlier, onehot, preferred_element_type=jnp.float32)
    slot_ids = jnp.sum(before * onehot.astype(jnp.float32), axis=2).astype(jnp.int32)
    rows = exp_dev * senders * capacity
    position = (pair_routes % exp_dev * senders + pair_routes // exp_dev) * capacity + slot_ids
    position = position.reshape(groups, token_count, top_count)
    row_ids = jnp.arange(rows, dtype=jnp.int32)
    select = (position[..., None] == row_ids).astype(jnp.bfloat16)
    gate_rows = all_gates.reshape(groups, token_count, top_count).astype(jnp.float32)
    gate_table = jnp.einsum("gtk,gtkr->gr", gate_rows, select.astype(jnp.float32))
    token_select = jnp.sum(select, axis=2)
    token_select = token_select.reshape(groups, token_count, exp_dev, senders, capacity)
    token_columns = columns.reshape(groups, token_count, quarter)
    gate_table = (
        gate_table.reshape(groups, exp_dev, senders, capacity).transpose(1, 0, 2, 3).astype(gates.dtype)
    )
    got_gates = lax.all_to_all(gate_table, "expert", split_axis=2, concat_axis=2, tiled=True)
    got_gates = got_gates.reshape(exp_dev, groups, slot_rows_all)
    slot_gates = got_gates.astype(jnp.float32)
    me = lax.axis_index("dp")
    own_gates = lax.dynamic_index_in_dim(got_gates, me, 1, keepdims=False).astype(jnp.float32)
    chunks = 2 if exp_dev % 2 == 0 else 1
    per = exp_dev // chunks
    grads, dots, hidden_parts = [], [], []
    incoming, partials = [], []
    for c in range(chunks):
        local = slice(c * per, (c + 1) * per)
        picked = jnp.einsum(
            "gtlqs,gtd->qglsd",
            token_select[:, :, local],
            token_columns,
            preferred_element_type=jnp.float32,
        ).astype(columns.dtype)
        received = lax.all_to_all(picked, "expert", split_axis=0, concat_axis=0, tiled=True)
        incoming.append(received)
        partials.append(
            jnp.einsum(
                "qglsd,lfd->glqsf", received, down_weight[local], preferred_element_type=jnp.float32
            ).reshape(groups, per, slot_rows_all, ff_part)
        )
    partials = list(lax.optimization_barrier(tuple(partials)))
    for c in range(chunks):
        local = slice(c * per, (c + 1) * per)
        partial, received = partials[c], incoming[c]
        sent = partial.astype(jnp.bfloat16)
        expert_grad = lax.dynamic_index_in_dim(partial, me, 0, keepdims=False)
        for shift in range(1, groups):
            chunk = lax.dynamic_index_in_dim(sent, (me + shift) % groups, 0, keepdims=False)
            pairs = [(i, (i + shift) % groups) for i in range(groups)]
            expert_grad = expert_grad + lax.ppermute(chunk, "dp", pairs).astype(jnp.float32)
        hidden_rows = hidden_all[:, local].astype(jnp.float32)
        dots.append(jnp.sum(hidden_rows * partial, axis=3))
        scaled = (jnp.moveaxis(slot_gates[local], 0, 1)[..., None] * hidden_rows).astype(jnp.bfloat16)
        scaled = scaled.reshape(groups, per, senders, capacity, ff_part)
        weight_sum = jnp.einsum("glqsf,qglsd->lfd", scaled, received, preferred_element_type=jnp.float32)
        grads.append(weight_sum.astype(jnp.bfloat16))
        hidden_parts.append((own_gates[local][..., None] * expert_grad).astype(jnp.bfloat16))
    weight_grad = jnp.concatenate(grads, axis=0)
    dot_part = jnp.concatenate(dots, axis=1)
    hidden_grad = jnp.concatenate(hidden_parts, axis=0)[None]
    own_dots = lax.dynamic_index_in_dim(dot_part, me, 0, keepdims=False)
    for shift in range(1, groups):
        chunk = lax.dynamic_index_in_dim(dot_part, (me + shift) % groups, 0, keepdims=False)
        pairs = [(i, (i + shift) % groups) for i in range(groups)]
        own_dots = own_dots + lax.ppermute(chunk, "dp", pairs)
    halves = lax.axis_size("etp")
    half_dots = own_dots
    for shift in range(1, halves):
        pairs = [(i, (i + shift) % halves) for i in range(halves)]
        own_dots = own_dots + lax.ppermute(half_dots, "etp", pairs)
    hidden_grad, own_dots, weight_grad = lax.optimization_barrier((hidden_grad, own_dots, weight_grad))
    slot_dots = own_dots.reshape(exp_dev, senders, capacity)
    returned = lax.all_to_all(slot_dots, "expert", split_axis=1, concat_axis=1, tiled=True)
    own_select = lax.dynamic_index_in_dim(select, me, 0, keepdims=False).astype(jnp.float32)
    gate_grad = jnp.sum(own_select * returned.reshape(1, 1, rows), axis=2)
    return (weight_grad, hidden_grad, gate_grad)


def solution(mesh):
    in_specs = (
        P(("dp", "expert"), None),
        P(("dp", "expert"), None),
        P(("dp", "expert"), None),
        P("dp", "expert", None, "etp"),
        P("expert", "etp", "dp"),
    )
    out_specs = (
        P("expert", "etp", "dp"),
        P("dp", "expert", None, "etp"),
        P(("dp", "expert"), None),
    )
    return jax.shard_map(body, mesh=mesh, in_specs=in_specs, out_specs=out_specs, check_vma=False)
```

```python
import jax
import jax.numpy as jnp
from jax import lax
from jax.sharding import PartitionSpec as P


def body(grad_out, routes, gates, hidden_saved, down_weight):
    token_count = grad_out.shape[0]
    top_count = routes.shape[1]
    exp_dev, ff_part, quarter = down_weight.shape
    groups = lax.axis_size("dp")
    senders = lax.axis_size("expert")
    slot_rows_all = hidden_saved.shape[2]
    capacity = slot_rows_all // senders
    experts = exp_dev * senders
    meta = jnp.concatenate([routes.astype(jnp.float32), gates.astype(jnp.float32)], axis=1)
    all_meta = lax.all_gather(meta, "dp", axis=0, tiled=True)
    columns = lax.all_to_all(grad_out, "dp", split_axis=1, concat_axis=0, tiled=True)
    hidden_saved, all_meta, columns = lax.optimization_barrier((hidden_saved, all_meta, columns))
    hidden_all = lax.all_gather(hidden_saved, "dp", axis=0, tiled=True)
    all_routes = all_meta[:, :top_count].astype(jnp.int32)
    all_gates = all_meta[:, top_count:].astype(gates.dtype)
    pair_count = token_count * top_count
    pair_routes = all_routes.reshape(groups, pair_count)
    expert_ids = jnp.arange(experts, dtype=jnp.int32)
    onehot = (pair_routes[:, :, None] == expert_ids[None, None, :]).astype(jnp.bfloat16)
    pair_ids = jnp.arange(pair_count, dtype=jnp.int32)
    earlier = (pair_ids[:, None] > pair_ids[None, :]).astype(jnp.bfloat16)
    before = jnp.einsum("jk,gke->gje", earlier, onehot, preferred_element_type=jnp.float32)
    slot_ids = jnp.sum(before * onehot.astype(jnp.float32), axis=2).astype(jnp.int32)
    rows = exp_dev * senders * capacity
    position = (pair_routes % exp_dev * senders + pair_routes // exp_dev) * capacity + slot_ids
    position = position.reshape(groups, token_count, top_count)
    row_ids = jnp.arange(rows, dtype=jnp.int32)
    select = (position[..., None] == row_ids).astype(jnp.bfloat16)
    gate_rows = all_gates.reshape(groups, token_count, top_count).astype(jnp.float32)
    gate_table = jnp.einsum("gtk,gtkr->gr", gate_rows, select.astype(jnp.float32))
    token_select = jnp.sum(select, axis=2)
    token_select = token_select.reshape(groups, token_count, exp_dev, senders, capacity)
    token_columns = columns.reshape(groups, token_count, quarter)
    gate_table = (
        gate_table.reshape(groups, exp_dev, senders, capacity).transpose(1, 0, 2, 3).astype(gates.dtype)
    )
    got_gates = lax.all_to_all(gate_table, "expert", split_axis=2, concat_axis=2, tiled=True)
    got_gates = got_gates.reshape(exp_dev, groups, slot_rows_all)
    slot_gates = got_gates.astype(jnp.float32)
    me = lax.axis_index("dp")
    own_gates = lax.dynamic_index_in_dim(got_gates, me, 1, keepdims=False).astype(jnp.float32)
    chunks = 2 if exp_dev % 2 == 0 else 1
    per = exp_dev // chunks
    grads, dots, hidden_parts = [], [], []
    for c in range(chunks):
        local = slice(c * per, (c + 1) * per)
        picked = jnp.einsum(
            "gtlqs,gtd->qglsd",
            token_select[:, :, local],
            token_columns,
            preferred_element_type=jnp.float32,
        ).astype(columns.dtype)
        received = lax.all_to_all(picked, "expert", split_axis=0, concat_axis=0, tiled=True)
        partial = jnp.einsum(
            "qglsd,lfd->glqsf", received, down_weight[local], preferred_element_type=jnp.float32
        ).reshape(groups, per, slot_rows_all, ff_part)
        sent = partial.astype(jnp.bfloat16)
        expert_grad = lax.dynamic_index_in_dim(partial, me, 0, keepdims=False)
        for shift in range(1, groups):
            chunk = lax.dynamic_index_in_dim(sent, (me + shift) % groups, 0, keepdims=False)
            pairs = [(i, (i + shift) % groups) for i in range(groups)]
            expert_grad = expert_grad + lax.ppermute(chunk, "dp", pairs).astype(jnp.float32)
        hidden_rows = hidden_all[:, local].astype(jnp.float32)
        dots.append(jnp.sum(hidden_rows * partial, axis=3))
        scaled = (jnp.moveaxis(slot_gates[local], 0, 1)[..., None] * hidden_rows).astype(jnp.bfloat16)
        scaled = scaled.reshape(groups, per, senders, capacity, ff_part)
        weight_sum = jnp.einsum("glqsf,qglsd->lfd", scaled, received, preferred_element_type=jnp.float32)
        grads.append(weight_sum.astype(jnp.bfloat16))
        hidden_parts.append((own_gates[local][..., None] * expert_grad).astype(jnp.bfloat16))
    weight_grad = jnp.concatenate(grads, axis=0)
    dot_part = jnp.concatenate(dots, axis=1)
    hidden_grad = jnp.concatenate(hidden_parts, axis=0)[None]
    own_dots = lax.dynamic_index_in_dim(dot_part, me, 0, keepdims=False)
    for shift in range(1, groups):
        chunk = lax.dynamic_index_in_dim(dot_part, (me + shift) % groups, 0, keepdims=False)
        pairs = [(i, (i + shift) % groups) for i in range(groups)]
        own_dots = own_dots + lax.ppermute(chunk, "dp", pairs)
    halves = lax.axis_size("etp")
    half_dots = own_dots
    for shift in range(1, halves):
        pairs = [(i, (i + shift) % halves) for i in range(halves)]
        own_dots = own_dots + lax.ppermute(half_dots, "etp", pairs)
    hidden_grad, own_dots, weight_grad = lax.optimization_barrier((hidden_grad, own_dots, weight_grad))
    slot_dots = own_dots.reshape(exp_dev, senders, capacity)
    returned = lax.all_to_all(slot_dots, "expert", split_axis=1, concat_axis=1, tiled=True)
    own_select = lax.dynamic_index_in_dim(select, me, 0, keepdims=False).astype(jnp.float32)
    gate_grad = jnp.sum(own_select * returned.reshape(1, 1, rows), axis=2)
    return (weight_grad, hidden_grad, gate_grad)


def solution(mesh):
    in_specs = (
        P(("dp", "expert"), None),
        P(("dp", "expert"), None),
        P(("dp", "expert"), None),
        P("dp", "expert", None, "etp"),
        P("expert", "etp", "dp"),
    )
    out_specs = (
        P("expert", "etp", "dp"),
        P("dp", "expert", None, "etp"),
        P(("dp", "expert"), None),
    )
    return jax.shard_map(body, mesh=mesh, in_specs=in_specs, out_specs=out_specs, check_vma=False)
```

```python
import jax
import jax.numpy as jnp
from jax import lax
from jax.sharding import PartitionSpec as P


def body(grad_out, routes, gates, hidden_saved, down_weight):
    token_count = grad_out.shape[0]
    top_count = routes.shape[1]
    exp_dev, ff_part, quarter = down_weight.shape
    groups = lax.axis_size("dp")
    senders = lax.axis_size("expert")
    slot_rows_all = hidden_saved.shape[2]
    capacity = slot_rows_all // senders
    experts = exp_dev * senders
    quarter_cols = grad_out.shape[1] // groups
    meta = jnp.concatenate([routes.astype(grad_out.dtype), gates.astype(grad_out.dtype)], axis=1)
    packed = jnp.concatenate(
        [
            grad_out.reshape(token_count, groups, quarter_cols),
            jnp.broadcast_to(meta[:, None, :], (token_count, groups, 2 * top_count)),
        ],
        axis=2,
    )
    moved = lax.all_to_all(packed, "dp", split_axis=1, concat_axis=0, tiled=True)
    hidden_saved, moved = lax.optimization_barrier((hidden_saved, moved))
    columns = moved[:, 0, :quarter_cols]
    all_meta = moved[:, 0, quarter_cols:]
    hidden_all = lax.all_gather(hidden_saved, "dp", axis=0, tiled=True)
    all_routes = all_meta[:, :top_count].astype(jnp.int32)
    all_gates = all_meta[:, top_count:].astype(gates.dtype)
    pair_count = token_count * top_count
    pair_routes = all_routes.reshape(groups, pair_count)
    expert_ids = jnp.arange(experts, dtype=jnp.int32)
    onehot = (pair_routes[:, :, None] == expert_ids[None, None, :]).astype(jnp.bfloat16)
    pair_ids = jnp.arange(pair_count, dtype=jnp.int32)
    earlier = (pair_ids[:, None] > pair_ids[None, :]).astype(jnp.bfloat16)
    before = jnp.einsum("jk,gke->gje", earlier, onehot, preferred_element_type=jnp.float32)
    slot_ids = jnp.sum(before * onehot.astype(jnp.float32), axis=2).astype(jnp.int32)
    rows = exp_dev * senders * capacity
    position = (pair_routes % exp_dev * senders + pair_routes // exp_dev) * capacity + slot_ids
    position = position.reshape(groups, token_count, top_count)
    row_ids = jnp.arange(rows, dtype=jnp.int32)
    select = (position[..., None] == row_ids).astype(jnp.bfloat16)
    gate_rows = all_gates.reshape(groups, token_count, top_count).astype(jnp.float32)
    gate_table = jnp.einsum("gtk,gtkr->gr", gate_rows, select.astype(jnp.float32))
    token_select = jnp.sum(select, axis=2)
    token_select = token_select.reshape(groups, token_count, exp_dev, senders, capacity)
    token_columns = columns.reshape(groups, token_count, quarter)
    gate_table = (
        gate_table.reshape(groups, exp_dev, senders, capacity).transpose(1, 0, 2, 3).astype(gates.dtype)
    )
    got_gates = lax.all_to_all(gate_table, "expert", split_axis=2, concat_axis=2, tiled=True)
    got_gates = got_gates.reshape(exp_dev, groups, slot_rows_all)
    slot_gates = got_gates.astype(jnp.float32)
    me = lax.axis_index("dp")
    own_gates = lax.dynamic_index_in_dim(got_gates, me, 1, keepdims=False).astype(jnp.float32)
    chunks = 2 if exp_dev % 2 == 0 else 1
    per = exp_dev // chunks
    grads, dots, hidden_parts = [], [], []
    for c in range(chunks):
        local = slice(c * per, (c + 1) * per)
        picked = jnp.einsum(
            "gtlqs,gtd->qglsd",
            token_select[:, :, local],
            token_columns,
            preferred_element_type=jnp.float32,
        ).astype(columns.dtype)
        received = lax.all_to_all(picked, "expert", split_axis=0, concat_axis=0, tiled=True)
        if c == chunks - 1:
            hidden_all, received = lax.optimization_barrier((hidden_all, received))
        partial = jnp.einsum(
            "qglsd,lfd->glqsf", received, down_weight[local], preferred_element_type=jnp.float32
        ).reshape(groups, per, slot_rows_all, ff_part)
        sent = partial.astype(jnp.bfloat16)
        expert_grad = lax.dynamic_index_in_dim(partial, me, 0, keepdims=False)
        for shift in range(1, groups):
            chunk = lax.dynamic_index_in_dim(sent, (me + shift) % groups, 0, keepdims=False)
            pairs = [(i, (i + shift) % groups) for i in range(groups)]
            expert_grad = expert_grad + lax.ppermute(chunk, "dp", pairs).astype(jnp.float32)
        hidden_rows = hidden_all[:, local].astype(jnp.float32)
        dots.append(jnp.sum(hidden_rows * partial, axis=3))
        scaled = (jnp.moveaxis(slot_gates[local], 0, 1)[..., None] * hidden_rows).astype(jnp.bfloat16)
        scaled = scaled.reshape(groups, per, senders, capacity, ff_part)
        weight_sum = jnp.einsum("glqsf,qglsd->lfd", scaled, received, preferred_element_type=jnp.float32)
        grads.append(weight_sum.astype(jnp.bfloat16))
        hidden_parts.append((own_gates[local][..., None] * expert_grad).astype(jnp.bfloat16))
    weight_grad = jnp.concatenate(grads, axis=0)
    dot_part = jnp.concatenate(dots, axis=1)
    hidden_grad = jnp.concatenate(hidden_parts, axis=0)[None]
    own_dots = lax.dynamic_index_in_dim(dot_part, me, 0, keepdims=False)
    for shift in range(1, groups):
        chunk = lax.dynamic_index_in_dim(dot_part, (me + shift) % groups, 0, keepdims=False)
        pairs = [(i, (i + shift) % groups) for i in range(groups)]
        own_dots = own_dots + lax.ppermute(chunk, "dp", pairs)
    halves = lax.axis_size("etp")
    half_dots = own_dots
    for shift in range(1, halves):
        pairs = [(i, (i + shift) % halves) for i in range(halves)]
        own_dots = own_dots + lax.ppermute(half_dots, "etp", pairs)
    hidden_grad, own_dots, weight_grad = lax.optimization_barrier((hidden_grad, own_dots, weight_grad))
    slot_dots = own_dots.reshape(exp_dev, senders, capacity)
    returned = lax.all_to_all(slot_dots, "expert", split_axis=1, concat_axis=1, tiled=True)
    own_select = lax.dynamic_index_in_dim(select, me, 0, keepdims=False).astype(jnp.float32)
    gate_grad = jnp.sum(own_select * returned.reshape(1, 1, rows), axis=2)
    return (weight_grad, hidden_grad, gate_grad)


def solution(mesh):
    in_specs = (
        P(("dp", "expert"), None),
        P(("dp", "expert"), None),
        P(("dp", "expert"), None),
        P("dp", "expert", None, "etp"),
        P("expert", "etp", "dp"),
    )
    out_specs = (
        P("expert", "etp", "dp"),
        P("dp", "expert", None, "etp"),
        P(("dp", "expert"), None),
    )
    return jax.shard_map(body, mesh=mesh, in_specs=in_specs, out_specs=out_specs, check_vma=False)
```

```python
import jax
import jax.numpy as jnp
from jax import lax
from jax.sharding import PartitionSpec as P


def body(grad_out, routes, gates, hidden_saved, down_weight):
    token_count = grad_out.shape[0]
    top_count = routes.shape[1]
    exp_dev, ff_part, quarter = down_weight.shape
    groups = lax.axis_size("dp")
    senders = lax.axis_size("expert")
    slot_rows_all = hidden_saved.shape[2]
    capacity = slot_rows_all // senders
    experts = exp_dev * senders
    quarter_cols = grad_out.shape[1] // groups
    meta = jnp.concatenate([routes.astype(grad_out.dtype), gates.astype(grad_out.dtype)], axis=1)
    packed = jnp.concatenate(
        [
            grad_out.reshape(token_count, groups, quarter_cols),
            jnp.broadcast_to(meta[:, None, :], (token_count, groups, 2 * top_count)),
        ],
        axis=2,
    )
    moved = lax.all_to_all(packed, "dp", split_axis=1, concat_axis=0, tiled=True)
    hidden_saved, moved = lax.optimization_barrier((hidden_saved, moved))
    columns = moved[:, 0, :quarter_cols]
    all_meta = moved[:, 0, quarter_cols:]
    hidden_all = lax.all_gather(hidden_saved, "dp", axis=0, tiled=True)
    all_routes = all_meta[:, :top_count].astype(jnp.int32)
    all_gates = all_meta[:, top_count:].astype(gates.dtype)
    pair_count = token_count * top_count
    pair_routes = all_routes.reshape(groups, pair_count)
    expert_ids = jnp.arange(experts, dtype=jnp.int32)
    onehot = (pair_routes[:, :, None] == expert_ids[None, None, :]).astype(jnp.bfloat16)
    pair_ids = jnp.arange(pair_count, dtype=jnp.int32)
    earlier = (pair_ids[:, None] > pair_ids[None, :]).astype(jnp.bfloat16)
    before = jnp.einsum("jk,gke->gje", earlier, onehot, preferred_element_type=jnp.float32)
    slot_ids = jnp.sum(before * onehot.astype(jnp.float32), axis=2).astype(jnp.int32)
    rows = exp_dev * senders * capacity
    position = (pair_routes % exp_dev * senders + pair_routes // exp_dev) * capacity + slot_ids
    position = position.reshape(groups, token_count, top_count)
    row_ids = jnp.arange(rows, dtype=jnp.int32)
    select = (position[..., None] == row_ids).astype(jnp.bfloat16)
    gate_rows = all_gates.reshape(groups, token_count, top_count).astype(jnp.float32)
    gate_table = jnp.einsum("gtk,gtkr->gr", gate_rows, select.astype(jnp.float32))
    token_select = jnp.sum(select, axis=2)
    token_select = token_select.reshape(groups, token_count, exp_dev, senders, capacity)
    token_columns = columns.reshape(groups, token_count, quarter)
    gate_table = (
        gate_table.reshape(groups, exp_dev, senders, capacity).transpose(1, 0, 2, 3).astype(gates.dtype)
    )
    got_gates = lax.all_to_all(gate_table, "expert", split_axis=2, concat_axis=2, tiled=True)
    got_gates = got_gates.reshape(exp_dev, groups, slot_rows_all)
    slot_gates = got_gates.astype(jnp.float32)
    me = lax.axis_index("dp")
    own_gates = lax.dynamic_index_in_dim(got_gates, me, 1, keepdims=False).astype(jnp.float32)
    chunks = 2 if exp_dev % 2 == 0 else 1
    per = exp_dev // chunks
    grads, dots, hidden_parts = [], [], []
    for c in range(chunks):
        local = slice(c * per, (c + 1) * per)
        picked = jnp.einsum(
            "gtlqs,gtd->qglsd",
            token_select[:, :, local],
            token_columns,
            preferred_element_type=jnp.float32,
        ).astype(columns.dtype)
        received = lax.all_to_all(picked, "expert", split_axis=0, concat_axis=0, tiled=True)
        partial = jnp.einsum(
            "qglsd,lfd->glqsf", received, down_weight[local], preferred_element_type=jnp.float32
        ).reshape(groups, per, slot_rows_all, ff_part)
        if c == chunks - 1:
            hidden_all, partial = lax.optimization_barrier((hidden_all, partial))
        sent = partial.astype(jnp.bfloat16)
        expert_grad = lax.dynamic_index_in_dim(partial, me, 0, keepdims=False)
        for shift in range(1, groups):
            chunk = lax.dynamic_index_in_dim(sent, (me + shift) % groups, 0, keepdims=False)
            pairs = [(i, (i + shift) % groups) for i in range(groups)]
            expert_grad = expert_grad + lax.ppermute(chunk, "dp", pairs).astype(jnp.float32)
        hidden_rows = hidden_all[:, local].astype(jnp.float32)
        dots.append(jnp.sum(hidden_rows * partial, axis=3))
        scaled = (jnp.moveaxis(slot_gates[local], 0, 1)[..., None] * hidden_rows).astype(jnp.bfloat16)
        scaled = scaled.reshape(groups, per, senders, capacity, ff_part)
        weight_sum = jnp.einsum("glqsf,qglsd->lfd", scaled, received, preferred_element_type=jnp.float32)
        grads.append(weight_sum.astype(jnp.bfloat16))
        hidden_parts.append((own_gates[local][..., None] * expert_grad).astype(jnp.bfloat16))
    weight_grad = jnp.concatenate(grads, axis=0)
    dot_part = jnp.concatenate(dots, axis=1)
    hidden_grad = jnp.concatenate(hidden_parts, axis=0)[None]
    own_dots = lax.dynamic_index_in_dim(dot_part, me, 0, keepdims=False)
    for shift in range(1, groups):
        chunk = lax.dynamic_index_in_dim(dot_part, (me + shift) % groups, 0, keepdims=False)
        pairs = [(i, (i + shift) % groups) for i in range(groups)]
        own_dots = own_dots + lax.ppermute(chunk, "dp", pairs)
    halves = lax.axis_size("etp")
    half_dots = own_dots
    for shift in range(1, halves):
        pairs = [(i, (i + shift) % halves) for i in range(halves)]
        own_dots = own_dots + lax.ppermute(half_dots, "etp", pairs)
    hidden_grad, own_dots, weight_grad = lax.optimization_barrier((hidden_grad, own_dots, weight_grad))
    slot_dots = own_dots.reshape(exp_dev, senders, capacity)
    returned = lax.all_to_all(slot_dots, "expert", split_axis=1, concat_axis=1, tiled=True)
    own_select = lax.dynamic_index_in_dim(select, me, 0, keepdims=False).astype(jnp.float32)
    gate_grad = jnp.sum(own_select * returned.reshape(1, 1, rows), axis=2)
    return (weight_grad, hidden_grad, gate_grad)


def solution(mesh):
    in_specs = (
        P(("dp", "expert"), None),
        P(("dp", "expert"), None),
        P(("dp", "expert"), None),
        P("dp", "expert", None, "etp"),
        P("expert", "etp", "dp"),
    )
    out_specs = (
        P("expert", "etp", "dp"),
        P("dp", "expert", None, "etp"),
        P(("dp", "expert"), None),
    )
    return jax.shard_map(body, mesh=mesh, in_specs=in_specs, out_specs=out_specs, check_vma=False)
```

```python
import jax
import jax.numpy as jnp
from jax import lax
from jax.sharding import PartitionSpec as P


def body(grad_out, routes, gates, hidden_saved, down_weight):
    token_count = grad_out.shape[0]
    top_count = routes.shape[1]
    exp_dev, ff_part, quarter = down_weight.shape
    groups = lax.axis_size("dp")
    senders = lax.axis_size("expert")
    slot_rows_all = hidden_saved.shape[2]
    capacity = slot_rows_all // senders
    experts = exp_dev * senders
    quarter_cols = grad_out.shape[1] // groups
    meta = jnp.concatenate([routes.astype(grad_out.dtype), gates.astype(grad_out.dtype)], axis=1)
    packed = jnp.concatenate(
        [
            grad_out.reshape(token_count, groups, quarter_cols),
            jnp.broadcast_to(meta[:, None, :], (token_count, groups, 2 * top_count)),
        ],
        axis=2,
    )
    moved = lax.all_to_all(packed, "dp", split_axis=1, concat_axis=0, tiled=True)
    hidden_saved, moved = lax.optimization_barrier((hidden_saved, moved))
    columns = moved[:, 0, :quarter_cols]
    all_meta = moved[:, 0, quarter_cols:]
    hidden_all = lax.all_gather(hidden_saved, "dp", axis=0, tiled=True)
    all_routes = all_meta[:, :top_count].astype(jnp.int32)
    all_gates = all_meta[:, top_count:].astype(gates.dtype)
    pair_count = token_count * top_count
    pair_routes = all_routes.reshape(groups, pair_count)
    expert_ids = jnp.arange(experts, dtype=jnp.int32)
    onehot = (pair_routes[:, :, None] == expert_ids[None, None, :]).astype(jnp.bfloat16)
    pair_ids = jnp.arange(pair_count, dtype=jnp.int32)
    earlier = (pair_ids[:, None] > pair_ids[None, :]).astype(jnp.bfloat16)
    before = jnp.einsum("jk,gke->gje", earlier, onehot, preferred_element_type=jnp.float32)
    slot_ids = jnp.sum(before * onehot.astype(jnp.float32), axis=2).astype(jnp.int32)
    rows = exp_dev * senders * capacity
    position = (pair_routes % exp_dev * senders + pair_routes // exp_dev) * capacity + slot_ids
    position = position.reshape(groups, token_count, top_count)
    row_ids = jnp.arange(rows, dtype=jnp.int32)
    select = (position[..., None] == row_ids).astype(jnp.bfloat16)
    gate_rows = all_gates.reshape(groups, token_count, top_count).astype(jnp.float32)
    gate_table = jnp.einsum("gtk,gtkr->gr", gate_rows, select.astype(jnp.float32))
    token_select = jnp.sum(select, axis=2)
    token_select = token_select.reshape(groups, token_count, exp_dev, senders, capacity)
    token_columns = columns.reshape(groups, token_count, quarter)
    gate_table = (
        gate_table.reshape(groups, exp_dev, senders, capacity).transpose(1, 0, 2, 3).astype(gates.dtype)
    )
    got_gates = lax.all_to_all(gate_table, "expert", split_axis=2, concat_axis=2, tiled=True)
    got_gates = got_gates.reshape(exp_dev, groups, slot_rows_all)
    slot_gates = got_gates.astype(jnp.float32)
    me = lax.axis_index("dp")
    own_gates = lax.dynamic_index_in_dim(got_gates, me, 1, keepdims=False).astype(jnp.float32)
    chunks = 2 if exp_dev % 2 == 0 else 1
    per = exp_dev // chunks
    grads, dots, hidden_parts = [], [], []
    for c in range(chunks):
        local = slice(c * per, (c + 1) * per)
        picked = jnp.einsum(
            "gtlqs,gtd->qglsd",
            token_select[:, :, local],
            token_columns,
            preferred_element_type=jnp.float32,
        ).astype(columns.dtype)
        received = lax.all_to_all(picked, "expert", split_axis=0, concat_axis=0, tiled=True)
        partial = jnp.einsum(
            "qglsd,lfd->glqsf", received, down_weight[local], preferred_element_type=jnp.float32
        ).reshape(groups, per, slot_rows_all, ff_part)
        if c == chunks - 1:
            hidden_all, partial = lax.optimization_barrier((hidden_all, partial))
        sent = partial.astype(jnp.bfloat16)
        arrivals = []
        for shift in range(1, groups):
            chunk = lax.dynamic_index_in_dim(sent, (me + shift) % groups, 0, keepdims=False)
            pairs = [(i, (i + shift) % groups) for i in range(groups)]
            arrivals.append(lax.ppermute(chunk, "dp", pairs))
        hidden_rows = hidden_all[:, local].astype(jnp.float32)
        dots.append(jnp.sum(hidden_rows * partial, axis=3))
        scaled = (jnp.moveaxis(slot_gates[local], 0, 1)[..., None] * hidden_rows).astype(jnp.bfloat16)
        scaled = scaled.reshape(groups, per, senders, capacity, ff_part)
        weight_sum = jnp.einsum("glqsf,qglsd->lfd", scaled, received, preferred_element_type=jnp.float32)
        grads.append(weight_sum.astype(jnp.bfloat16))
        expert_grad = lax.dynamic_index_in_dim(partial, me, 0, keepdims=False)
        if c == chunks - 1:
            weight_grad = jnp.concatenate(grads, axis=0)
            weight_grad, expert_grad = lax.optimization_barrier((weight_grad, expert_grad))
        for arrived in arrivals:
            expert_grad = expert_grad + arrived.astype(jnp.float32)
        hidden_parts.append((own_gates[local][..., None] * expert_grad).astype(jnp.bfloat16))
    dot_part = jnp.concatenate(dots, axis=1)
    hidden_grad = jnp.concatenate(hidden_parts, axis=0)[None]
    own_dots = lax.dynamic_index_in_dim(dot_part, me, 0, keepdims=False)
    for shift in range(1, groups):
        chunk = lax.dynamic_index_in_dim(dot_part, (me + shift) % groups, 0, keepdims=False)
        pairs = [(i, (i + shift) % groups) for i in range(groups)]
        own_dots = own_dots + lax.ppermute(chunk, "dp", pairs)
    halves = lax.axis_size("etp")
    half_dots = own_dots
    for shift in range(1, halves):
        pairs = [(i, (i + shift) % halves) for i in range(halves)]
        own_dots = own_dots + lax.ppermute(half_dots, "etp", pairs)
    hidden_grad, own_dots, weight_grad = lax.optimization_barrier((hidden_grad, own_dots, weight_grad))
    slot_dots = own_dots.reshape(exp_dev, senders, capacity)
    returned = lax.all_to_all(slot_dots, "expert", split_axis=1, concat_axis=1, tiled=True)
    own_select = lax.dynamic_index_in_dim(select, me, 0, keepdims=False).astype(jnp.float32)
    gate_grad = jnp.sum(own_select * returned.reshape(1, 1, rows), axis=2)
    return (weight_grad, hidden_grad, gate_grad)


def solution(mesh):
    in_specs = (
        P(("dp", "expert"), None),
        P(("dp", "expert"), None),
        P(("dp", "expert"), None),
        P("dp", "expert", None, "etp"),
        P("expert", "etp", "dp"),
    )
    out_specs = (
        P("expert", "etp", "dp"),
        P("dp", "expert", None, "etp"),
        P(("dp", "expert"), None),
    )
    return jax.shard_map(body, mesh=mesh, in_specs=in_specs, out_specs=out_specs, check_vma=False)
```

```python
import jax
import jax.numpy as jnp
from jax import lax
from jax.sharding import PartitionSpec as P


def body(grad_out, routes, gates, hidden_saved, down_weight):
    token_count = grad_out.shape[0]
    top_count = routes.shape[1]
    exp_dev, ff_part, quarter = down_weight.shape
    groups = lax.axis_size("dp")
    senders = lax.axis_size("expert")
    slot_rows_all = hidden_saved.shape[2]
    capacity = slot_rows_all // senders
    experts = exp_dev * senders
    quarter_cols = grad_out.shape[1] // groups
    meta = jnp.concatenate([routes.astype(grad_out.dtype), gates.astype(grad_out.dtype)], axis=1)
    packed = jnp.concatenate(
        [
            grad_out.reshape(token_count, groups, quarter_cols),
            jnp.broadcast_to(meta[:, None, :], (token_count, groups, 2 * top_count)),
        ],
        axis=2,
    )
    moved = lax.all_to_all(packed, "dp", split_axis=1, concat_axis=0, tiled=True)
    hidden_saved, moved = lax.optimization_barrier((hidden_saved, moved))
    columns = moved[:, 0, :quarter_cols]
    all_meta = moved[:, 0, quarter_cols:]
    hidden_all = lax.all_gather(hidden_saved, "dp", axis=0, tiled=True)
    all_routes = all_meta[:, :top_count].astype(jnp.int32)
    all_gates = all_meta[:, top_count:].astype(gates.dtype)
    pair_count = token_count * top_count
    pair_routes = all_routes.reshape(groups, pair_count)
    expert_ids = jnp.arange(experts, dtype=jnp.int32)
    onehot = (pair_routes[:, :, None] == expert_ids[None, None, :]).astype(jnp.bfloat16)
    pair_ids = jnp.arange(pair_count, dtype=jnp.int32)
    earlier = (pair_ids[:, None] > pair_ids[None, :]).astype(jnp.bfloat16)
    before = jnp.einsum("jk,gke->gje", earlier, onehot, preferred_element_type=jnp.float32)
    slot_ids = jnp.sum(before * onehot.astype(jnp.float32), axis=2).astype(jnp.int32)
    rows = exp_dev * senders * capacity
    position = (pair_routes % exp_dev * senders + pair_routes // exp_dev) * capacity + slot_ids
    position = position.reshape(groups, token_count, top_count)
    row_ids = jnp.arange(rows, dtype=jnp.int32)
    select = (position[..., None] == row_ids).astype(jnp.bfloat16)
    gate_rows = all_gates.reshape(groups, token_count, top_count).astype(jnp.float32)
    gate_table = jnp.einsum("gtk,gtkr->gr", gate_rows, select.astype(jnp.float32))
    token_select = jnp.sum(select, axis=2)
    token_select = token_select.reshape(groups, token_count, exp_dev, senders, capacity)
    token_columns = columns.reshape(groups, token_count, quarter)
    gate_table = (
        gate_table.reshape(groups, exp_dev, senders, capacity).transpose(1, 0, 2, 3).astype(gates.dtype)
    )
    got_gates = lax.all_to_all(gate_table, "expert", split_axis=2, concat_axis=2, tiled=True)
    got_gates = got_gates.reshape(exp_dev, groups, slot_rows_all)
    slot_gates = got_gates.astype(jnp.float32)
    me = lax.axis_index("dp")
    own_gates = lax.dynamic_index_in_dim(got_gates, me, 1, keepdims=False).astype(jnp.float32)
    chunks = 2 if exp_dev % 2 == 0 else 1
    per = exp_dev // chunks
    grads, dots, hidden_parts = [], [], []
    for c in range(chunks):
        local = slice(c * per, (c + 1) * per)
        picked = jnp.einsum(
            "gtlqs,gtd->qglsd",
            token_select[:, :, local],
            token_columns,
            preferred_element_type=jnp.float32,
        ).astype(columns.dtype)
        received = lax.all_to_all(picked, "expert", split_axis=0, concat_axis=0, tiled=True)
        partial = jnp.einsum(
            "qglsd,lfd->glqsf", received, down_weight[local], preferred_element_type=jnp.float32
        ).reshape(groups, per, slot_rows_all, ff_part)
        if c == chunks - 1:
            hidden_all, partial = lax.optimization_barrier((hidden_all, partial))
        sent = partial.astype(jnp.bfloat16)
        arrivals = []
        for shift in range(1, groups):
            chunk = lax.dynamic_index_in_dim(sent, (me + shift) % groups, 0, keepdims=False)
            pairs = [(i, (i + shift) % groups) for i in range(groups)]
            arrivals.append(lax.ppermute(chunk, "dp", pairs))
        hidden_rows = hidden_all[:, local].astype(jnp.float32)
        dots.append(jnp.sum(hidden_rows * partial, axis=3))
        scaled = (jnp.moveaxis(slot_gates[local], 0, 1)[..., None] * hidden_rows).astype(jnp.bfloat16)
        scaled = scaled.reshape(groups, per, senders, capacity, ff_part)
        weight_sum = jnp.einsum("glqsf,qglsd->lfd", scaled, received, preferred_element_type=jnp.float32)
        grads.append(weight_sum.astype(jnp.bfloat16))
        expert_grad = lax.dynamic_index_in_dim(partial, me, 0, keepdims=False)
        if c == chunks - 1:
            weight_grad = jnp.concatenate(grads, axis=0)
            own_select = lax.dynamic_index_in_dim(select, me, 0, keepdims=False).astype(jnp.float32)
            weight_grad, expert_grad, own_select = lax.optimization_barrier(
                (weight_grad, expert_grad, own_select)
            )
        for arrived in arrivals:
            expert_grad = expert_grad + arrived.astype(jnp.float32)
        hidden_parts.append((own_gates[local][..., None] * expert_grad).astype(jnp.bfloat16))
    dot_part = jnp.concatenate(dots, axis=1)
    hidden_grad = jnp.concatenate(hidden_parts, axis=0)[None]
    own_dots = lax.dynamic_index_in_dim(dot_part, me, 0, keepdims=False)
    for shift in range(1, groups):
        chunk = lax.dynamic_index_in_dim(dot_part, (me + shift) % groups, 0, keepdims=False)
        pairs = [(i, (i + shift) % groups) for i in range(groups)]
        own_dots = own_dots + lax.ppermute(chunk, "dp", pairs)
    halves = lax.axis_size("etp")
    half_dots = own_dots
    for shift in range(1, halves):
        pairs = [(i, (i + shift) % halves) for i in range(halves)]
        own_dots = own_dots + lax.ppermute(half_dots, "etp", pairs)
    hidden_grad, own_dots, weight_grad = lax.optimization_barrier((hidden_grad, own_dots, weight_grad))
    slot_dots = own_dots.reshape(exp_dev, senders, capacity)
    returned = lax.all_to_all(slot_dots, "expert", split_axis=1, concat_axis=1, tiled=True)
    gate_grad = jnp.sum(own_select * returned.reshape(1, 1, rows), axis=2)
    return (weight_grad, hidden_grad, gate_grad)


def solution(mesh):
    in_specs = (
        P(("dp", "expert"), None),
        P(("dp", "expert"), None),
        P(("dp", "expert"), None),
        P("dp", "expert", None, "etp"),
        P("expert", "etp", "dp"),
    )
    out_specs = (
        P("expert", "etp", "dp"),
        P("dp", "expert", None, "etp"),
        P(("dp", "expert"), None),
    )
    return jax.shard_map(body, mesh=mesh, in_specs=in_specs, out_specs=out_specs, check_vma=False)
```

```python
import jax
import jax.numpy as jnp
from jax import lax
from jax.sharding import PartitionSpec as P


def reduce_dots(dot_part, me, groups):
    own_dots = lax.dynamic_index_in_dim(dot_part, me, 0, keepdims=False)
    for shift in range(1, groups):
        chunk = lax.dynamic_index_in_dim(dot_part, (me + shift) % groups, 0, keepdims=False)
        pairs = [(i, (i + shift) % groups) for i in range(groups)]
        own_dots = own_dots + lax.ppermute(chunk, "dp", pairs)
    halves = lax.axis_size("etp")
    half_dots = own_dots
    for shift in range(1, halves):
        pairs = [(i, (i + shift) % halves) for i in range(halves)]
        own_dots = own_dots + lax.ppermute(half_dots, "etp", pairs)
    return own_dots


def body(grad_out, routes, gates, hidden_saved, down_weight):
    token_count = grad_out.shape[0]
    top_count = routes.shape[1]
    exp_dev, ff_part, quarter = down_weight.shape
    groups = lax.axis_size("dp")
    senders = lax.axis_size("expert")
    slot_rows_all = hidden_saved.shape[2]
    capacity = slot_rows_all // senders
    experts = exp_dev * senders
    quarter_cols = grad_out.shape[1] // groups
    meta = jnp.concatenate([routes.astype(grad_out.dtype), gates.astype(grad_out.dtype)], axis=1)
    packed = jnp.concatenate(
        [
            grad_out.reshape(token_count, groups, quarter_cols),
            jnp.broadcast_to(meta[:, None, :], (token_count, groups, 2 * top_count)),
        ],
        axis=2,
    )
    moved = lax.all_to_all(packed, "dp", split_axis=1, concat_axis=0, tiled=True)
    hidden_saved, moved = lax.optimization_barrier((hidden_saved, moved))
    columns = moved[:, 0, :quarter_cols]
    all_meta = moved[:, 0, quarter_cols:]
    hidden_all = lax.all_gather(hidden_saved, "dp", axis=0, tiled=True)
    all_routes = all_meta[:, :top_count].astype(jnp.int32)
    all_gates = all_meta[:, top_count:].astype(gates.dtype)
    pair_count = token_count * top_count
    pair_routes = all_routes.reshape(groups, pair_count)
    expert_ids = jnp.arange(experts, dtype=jnp.int32)
    onehot = (pair_routes[:, :, None] == expert_ids[None, None, :]).astype(jnp.bfloat16)
    pair_ids = jnp.arange(pair_count, dtype=jnp.int32)
    earlier = (pair_ids[:, None] > pair_ids[None, :]).astype(jnp.bfloat16)
    before = jnp.einsum("jk,gke->gje", earlier, onehot, preferred_element_type=jnp.float32)
    slot_ids = jnp.sum(before * onehot.astype(jnp.float32), axis=2).astype(jnp.int32)
    rows = exp_dev * senders * capacity
    position = (pair_routes % exp_dev * senders + pair_routes // exp_dev) * capacity + slot_ids
    position = position.reshape(groups, token_count, top_count)
    row_ids = jnp.arange(rows, dtype=jnp.int32)
    select = (position[..., None] == row_ids).astype(jnp.bfloat16)
    gate_rows = all_gates.reshape(groups, token_count, top_count).astype(jnp.float32)
    gate_table = jnp.einsum("gtk,gtkr->gr", gate_rows, select.astype(jnp.float32))
    token_select = jnp.sum(select, axis=2)
    token_select = token_select.reshape(groups, token_count, exp_dev, senders, capacity)
    token_columns = columns.reshape(groups, token_count, quarter)
    gate_table = (
        gate_table.reshape(groups, exp_dev, senders, capacity).transpose(1, 0, 2, 3).astype(gates.dtype)
    )
    got_gates = lax.all_to_all(gate_table, "expert", split_axis=2, concat_axis=2, tiled=True)
    got_gates = got_gates.reshape(exp_dev, groups, slot_rows_all)
    slot_gates = got_gates.astype(jnp.float32)
    me = lax.axis_index("dp")
    own_gates = lax.dynamic_index_in_dim(got_gates, me, 1, keepdims=False).astype(jnp.float32)
    chunks = 2 if exp_dev % 2 == 0 else 1
    per = exp_dev // chunks
    grads, dots, hidden_parts = [], [], []
    for c in range(chunks):
        local = slice(c * per, (c + 1) * per)
        picked = jnp.einsum(
            "gtlqs,gtd->qglsd",
            token_select[:, :, local],
            token_columns,
            preferred_element_type=jnp.float32,
        ).astype(columns.dtype)
        received = lax.all_to_all(picked, "expert", split_axis=0, concat_axis=0, tiled=True)
        partial = jnp.einsum(
            "qglsd,lfd->glqsf", received, down_weight[local], preferred_element_type=jnp.float32
        ).reshape(groups, per, slot_rows_all, ff_part)
        if c == chunks - 1:
            hidden_all, partial = lax.optimization_barrier((hidden_all, partial))
        hidden_rows = hidden_all[:, local].astype(jnp.float32)
        dots.append(jnp.sum(hidden_rows * partial, axis=3))
        if c == chunks - 1:
            own_dots = reduce_dots(jnp.concatenate(dots, axis=1), me, groups)
            partial, own_dots = lax.optimization_barrier((partial, own_dots))
        sent = partial.astype(jnp.bfloat16)
        arrivals = []
        for shift in range(1, groups):
            chunk = lax.dynamic_index_in_dim(sent, (me + shift) % groups, 0, keepdims=False)
            pairs = [(i, (i + shift) % groups) for i in range(groups)]
            arrivals.append(lax.ppermute(chunk, "dp", pairs))
        scaled = (jnp.moveaxis(slot_gates[local], 0, 1)[..., None] * hidden_rows).astype(jnp.bfloat16)
        scaled = scaled.reshape(groups, per, senders, capacity, ff_part)
        weight_sum = jnp.einsum("glqsf,qglsd->lfd", scaled, received, preferred_element_type=jnp.float32)
        grads.append(weight_sum.astype(jnp.bfloat16))
        expert_grad = lax.dynamic_index_in_dim(partial, me, 0, keepdims=False)
        if c == chunks - 1:
            weight_grad = jnp.concatenate(grads, axis=0)
            own_select = lax.dynamic_index_in_dim(select, me, 0, keepdims=False).astype(jnp.float32)
            weight_grad, expert_grad, own_select = lax.optimization_barrier(
                (weight_grad, expert_grad, own_select)
            )
        for arrived in arrivals:
            expert_grad = expert_grad + arrived.astype(jnp.float32)
        hidden_parts.append((own_gates[local][..., None] * expert_grad).astype(jnp.bfloat16))
    hidden_grad = jnp.concatenate(hidden_parts, axis=0)[None]
    hidden_grad, own_dots, weight_grad = lax.optimization_barrier((hidden_grad, own_dots, weight_grad))
    slot_dots = own_dots.reshape(exp_dev, senders, capacity)
    returned = lax.all_to_all(slot_dots, "expert", split_axis=1, concat_axis=1, tiled=True)
    gate_grad = jnp.sum(own_select * returned.reshape(1, 1, rows), axis=2)
    return (weight_grad, hidden_grad, gate_grad)


def solution(mesh):
    in_specs = (
        P(("dp", "expert"), None),
        P(("dp", "expert"), None),
        P(("dp", "expert"), None),
        P("dp", "expert", None, "etp"),
        P("expert", "etp", "dp"),
    )
    out_specs = (
        P("expert", "etp", "dp"),
        P("dp", "expert", None, "etp"),
        P(("dp", "expert"), None),
    )
    return jax.shard_map(body, mesh=mesh, in_specs=in_specs, out_specs=out_specs, check_vma=False)
```

```python
import jax
import jax.numpy as jnp
from jax import lax
from jax.sharding import PartitionSpec as P


def body(grad_out, routes, gates, hidden_saved, down_weight):
    token_count = grad_out.shape[0]
    top_count = routes.shape[1]
    exp_dev, ff_part, quarter = down_weight.shape
    groups = lax.axis_size("dp")
    senders = lax.axis_size("expert")
    slot_rows_all = hidden_saved.shape[2]
    capacity = slot_rows_all // senders
    experts = exp_dev * senders
    quarter_cols = grad_out.shape[1] // groups
    meta = jnp.concatenate([routes.astype(grad_out.dtype), gates.astype(grad_out.dtype)], axis=1)
    packed = jnp.concatenate(
        [
            grad_out.reshape(token_count, groups, quarter_cols),
            jnp.broadcast_to(meta[:, None, :], (token_count, groups, 2 * top_count)),
        ],
        axis=2,
    )
    moved = lax.all_to_all(packed, "dp", split_axis=1, concat_axis=0, tiled=True)
    hidden_saved, moved = lax.optimization_barrier((hidden_saved, moved))
    columns = moved[:, 0, :quarter_cols]
    all_meta = moved[:, 0, quarter_cols:]
    hidden_all = lax.all_gather(hidden_saved, "dp", axis=0, tiled=True)
    all_routes = all_meta[:, :top_count].astype(jnp.int32)
    all_gates = all_meta[:, top_count:].astype(gates.dtype)
    pair_count = token_count * top_count
    pair_routes = all_routes.reshape(groups, pair_count)
    expert_ids = jnp.arange(experts, dtype=jnp.int32)
    onehot = (pair_routes[:, :, None] == expert_ids[None, None, :]).astype(jnp.bfloat16)
    pair_ids = jnp.arange(pair_count, dtype=jnp.int32)
    earlier = (pair_ids[:, None] > pair_ids[None, :]).astype(jnp.bfloat16)
    before = jnp.einsum("jk,gke->gje", earlier, onehot, preferred_element_type=jnp.float32)
    slot_ids = jnp.sum(before * onehot.astype(jnp.float32), axis=2).astype(jnp.int32)
    rows = exp_dev * senders * capacity
    position = (pair_routes % exp_dev * senders + pair_routes // exp_dev) * capacity + slot_ids
    position = position.reshape(groups, token_count, top_count)
    row_ids = jnp.arange(rows, dtype=jnp.int32)
    select = (position[..., None] == row_ids).astype(jnp.bfloat16)
    gate_rows = all_gates.reshape(groups, token_count, top_count).astype(jnp.float32)
    gate_table = jnp.einsum("gtk,gtkr->gr", gate_rows, select.astype(jnp.float32))
    token_select = jnp.sum(select, axis=2)
    token_select = token_select.reshape(groups, token_count, exp_dev, senders, capacity)
    token_columns = columns.reshape(groups, token_count, quarter)
    gate_table = (
        gate_table.reshape(groups, exp_dev, senders, capacity).transpose(1, 0, 2, 3).astype(gates.dtype)
    )
    got_gates = lax.all_to_all(gate_table, "expert", split_axis=2, concat_axis=2, tiled=True)
    got_gates = got_gates.reshape(exp_dev, groups, slot_rows_all)
    slot_gates = got_gates.astype(jnp.float32)
    me = lax.axis_index("dp")
    own_gates = lax.dynamic_index_in_dim(got_gates, me, 1, keepdims=False).astype(jnp.float32)
    chunks = 2 if exp_dev % 2 == 0 else 1
    per = exp_dev // chunks
    grads, dots, hidden_parts, owns, pending = [], [], [], [], []
    for c in range(chunks):
        local = slice(c * per, (c + 1) * per)
        picked = jnp.einsum(
            "gtlqs,gtd->qglsd",
            token_select[:, :, local],
            token_columns,
            preferred_element_type=jnp.float32,
        ).astype(columns.dtype)
        received = lax.all_to_all(picked, "expert", split_axis=0, concat_axis=0, tiled=True)
        partial = jnp.einsum(
            "qglsd,lfd->glqsf", received, down_weight[local], preferred_element_type=jnp.float32
        ).reshape(groups, per, slot_rows_all, ff_part)
        if c == chunks - 1:
            hidden_all, partial = lax.optimization_barrier((hidden_all, partial))
        sent = partial.astype(jnp.bfloat16)
        arrivals = []
        for shift in range(1, groups):
            chunk = lax.dynamic_index_in_dim(sent, (me + shift) % groups, 0, keepdims=False)
            pairs = [(i, (i + shift) % groups) for i in range(groups)]
            arrivals.append(lax.ppermute(chunk, "dp", pairs))
        hidden_rows = hidden_all[:, local].astype(jnp.float32)
        dots.append(jnp.sum(hidden_rows * partial, axis=3))
        scaled = (jnp.moveaxis(slot_gates[local], 0, 1)[..., None] * hidden_rows).astype(jnp.bfloat16)
        scaled = scaled.reshape(groups, per, senders, capacity, ff_part)
        weight_sum = jnp.einsum("glqsf,qglsd->lfd", scaled, received, preferred_element_type=jnp.float32)
        grads.append(weight_sum.astype(jnp.bfloat16))
        owns.append(lax.dynamic_index_in_dim(partial, me, 0, keepdims=False))
        pending.append(arrivals)
    weight_grad = jnp.concatenate(grads, axis=0)
    own_select = lax.dynamic_index_in_dim(select, me, 0, keepdims=False).astype(jnp.float32)
    weight_grad, owns, own_select = lax.optimization_barrier((weight_grad, tuple(owns), own_select))
    for c in range(chunks):
        local = slice(c * per, (c + 1) * per)
        expert_grad = owns[c]
        for arrived in pending[c]:
            expert_grad = expert_grad + arrived.astype(jnp.float32)
        hidden_parts.append((own_gates[local][..., None] * expert_grad).astype(jnp.bfloat16))
    dot_part = jnp.concatenate(dots, axis=1)
    hidden_grad = jnp.concatenate(hidden_parts, axis=0)[None]
    own_dots = lax.dynamic_index_in_dim(dot_part, me, 0, keepdims=False)
    for shift in range(1, groups):
        chunk = lax.dynamic_index_in_dim(dot_part, (me + shift) % groups, 0, keepdims=False)
        pairs = [(i, (i + shift) % groups) for i in range(groups)]
        own_dots = own_dots + lax.ppermute(chunk, "dp", pairs)
    halves = lax.axis_size("etp")
    half_dots = own_dots
    for shift in range(1, halves):
        pairs = [(i, (i + shift) % halves) for i in range(halves)]
        own_dots = own_dots + lax.ppermute(half_dots, "etp", pairs)
    hidden_grad, own_dots, weight_grad = lax.optimization_barrier((hidden_grad, own_dots, weight_grad))
    slot_dots = own_dots.reshape(exp_dev, senders, capacity)
    returned = lax.all_to_all(slot_dots, "expert", split_axis=1, concat_axis=1, tiled=True)
    gate_grad = jnp.sum(own_select * returned.reshape(1, 1, rows), axis=2)
    return (weight_grad, hidden_grad, gate_grad)


def solution(mesh):
    in_specs = (
        P(("dp", "expert"), None),
        P(("dp", "expert"), None),
        P(("dp", "expert"), None),
        P("dp", "expert", None, "etp"),
        P("expert", "etp", "dp"),
    )
    out_specs = (
        P("expert", "etp", "dp"),
        P("dp", "expert", None, "etp"),
        P(("dp", "expert"), None),
    )
    return jax.shard_map(body, mesh=mesh, in_specs=in_specs, out_specs=out_specs, check_vma=False)
```

```python
import jax
import jax.numpy as jnp
from jax import lax
from jax.sharding import PartitionSpec as P


def body(grad_out, routes, gates, hidden_saved, down_weight):
    token_count = grad_out.shape[0]
    top_count = routes.shape[1]
    exp_dev, ff_part, quarter = down_weight.shape
    groups = lax.axis_size("dp")
    senders = lax.axis_size("expert")
    slot_rows_all = hidden_saved.shape[2]
    capacity = slot_rows_all // senders
    experts = exp_dev * senders
    quarter_cols = grad_out.shape[1] // groups
    meta = jnp.concatenate([routes.astype(grad_out.dtype), gates.astype(grad_out.dtype)], axis=1)
    packed = jnp.concatenate(
        [
            grad_out.reshape(token_count, groups, quarter_cols),
            jnp.broadcast_to(meta[:, None, :], (token_count, groups, 2 * top_count)),
        ],
        axis=2,
    )
    moved = lax.all_to_all(packed, "dp", split_axis=1, concat_axis=0, tiled=True)
    hidden_saved, moved = lax.optimization_barrier((hidden_saved, moved))
    columns = moved[:, 0, :quarter_cols]
    all_meta = moved[:, 0, quarter_cols:]
    hidden_all = lax.all_gather(hidden_saved, "dp", axis=0, tiled=True)
    all_routes = all_meta[:, :top_count].astype(jnp.int32)
    all_gates = all_meta[:, top_count:].astype(gates.dtype)
    pair_count = token_count * top_count
    pair_routes = all_routes.reshape(groups, pair_count)
    expert_ids = jnp.arange(experts, dtype=jnp.int32)
    onehot = (pair_routes[:, :, None] == expert_ids[None, None, :]).astype(jnp.bfloat16)
    pair_ids = jnp.arange(pair_count, dtype=jnp.int32)
    earlier = (pair_ids[:, None] > pair_ids[None, :]).astype(jnp.bfloat16)
    before = jnp.einsum("jk,gke->gje", earlier, onehot, preferred_element_type=jnp.float32)
    slot_ids = jnp.sum(before * onehot.astype(jnp.float32), axis=2).astype(jnp.int32)
    rows = exp_dev * senders * capacity
    position = (pair_routes % exp_dev * senders + pair_routes // exp_dev) * capacity + slot_ids
    position = position.reshape(groups, token_count, top_count)
    row_ids = jnp.arange(rows, dtype=jnp.int32)
    select = (position[..., None] == row_ids).astype(jnp.bfloat16)
    gate_rows = all_gates.reshape(groups, token_count, top_count).astype(jnp.float32)
    gate_table = jnp.einsum("gtk,gtkr->gr", gate_rows, select.astype(jnp.float32))
    token_select = jnp.sum(select, axis=2)
    token_select = token_select.reshape(groups, token_count, exp_dev, senders, capacity)
    token_columns = columns.reshape(groups, token_count, quarter)
    gate_table = (
        gate_table.reshape(groups, exp_dev, senders, capacity).transpose(1, 0, 2, 3).astype(gates.dtype)
    )
    got_gates = lax.all_to_all(gate_table, "expert", split_axis=2, concat_axis=2, tiled=True)
    got_gates = got_gates.reshape(exp_dev, groups, slot_rows_all)
    slot_gates = got_gates.astype(jnp.float32)
    me = lax.axis_index("dp")
    own_gates = lax.dynamic_index_in_dim(got_gates, me, 1, keepdims=False).astype(jnp.float32)
    chunks = 2 if exp_dev % 2 == 0 else 1
    per = exp_dev // chunks
    grads, dots, hidden_parts = [], [], []
    for c in range(chunks):
        local = slice(c * per, (c + 1) * per)
        picked = jnp.einsum(
            "gtlqs,gtd->qglsd",
            token_select[:, :, local],
            token_columns,
            preferred_element_type=jnp.float32,
        ).astype(columns.dtype)
        received = lax.all_to_all(picked, "expert", split_axis=0, concat_axis=0, tiled=True)
        partial = jnp.einsum(
            "qglsd,lfd->glqsf", received, down_weight[local], preferred_element_type=jnp.float32
        ).reshape(groups, per, slot_rows_all, ff_part)
        if c == chunks - 1:
            hidden_all, partial = lax.optimization_barrier((hidden_all, partial))
        sent = partial.astype(jnp.bfloat16)
        arrivals = []
        for shift in range(1, groups):
            chunk = lax.dynamic_index_in_dim(sent, (me + shift) % groups, 0, keepdims=False)
            pairs = [(i, (i + shift) % groups) for i in range(groups)]
            arrivals.append(lax.ppermute(chunk, "dp", pairs))
        hidden_rows = hidden_all[:, local].astype(jnp.float32)
        dots.append(jnp.sum(hidden_rows * partial, axis=3))
        scaled = (jnp.moveaxis(slot_gates[local], 0, 1)[..., None] * hidden_rows).astype(jnp.bfloat16)
        scaled = scaled.reshape(groups, per, senders, capacity, ff_part)
        weight_sum = jnp.einsum("glqsf,qglsd->lfd", scaled, received, preferred_element_type=jnp.float32)
        grads.append(weight_sum.astype(jnp.bfloat16))
        expert_grad = lax.dynamic_index_in_dim(partial, me, 0, keepdims=False)
        if c == chunks - 1:
            weight_grad = jnp.concatenate(grads, axis=0)
            own_select = lax.dynamic_index_in_dim(select, me, 0, keepdims=False).astype(jnp.float32)
            weight_grad, expert_grad, own_select = lax.optimization_barrier(
                (weight_grad, expert_grad, own_select)
            )
        for arrived in arrivals:
            expert_grad = expert_grad + arrived.astype(jnp.float32)
        hidden_parts.append((own_gates[local][..., None] * expert_grad).astype(jnp.bfloat16))
    dot_part = jnp.concatenate(dots, axis=1)
    hidden_grad = jnp.concatenate(hidden_parts, axis=0)[None]
    halves = lax.axis_size("etp")
    half_dots = dot_part
    for shift in range(1, halves):
        pairs = [(i, (i + shift) % halves) for i in range(halves)]
        dot_part = dot_part + lax.ppermute(half_dots, "etp", pairs)
    own_dots = lax.dynamic_index_in_dim(dot_part, me, 0, keepdims=False)
    for shift in range(1, groups):
        chunk = lax.dynamic_index_in_dim(dot_part, (me + shift) % groups, 0, keepdims=False)
        pairs = [(i, (i + shift) % groups) for i in range(groups)]
        own_dots = own_dots + lax.ppermute(chunk, "dp", pairs)
    hidden_grad, own_dots, weight_grad = lax.optimization_barrier((hidden_grad, own_dots, weight_grad))
    slot_dots = own_dots.reshape(exp_dev, senders, capacity)
    returned = lax.all_to_all(slot_dots, "expert", split_axis=1, concat_axis=1, tiled=True)
    gate_grad = jnp.sum(own_select * returned.reshape(1, 1, rows), axis=2)
    return (weight_grad, hidden_grad, gate_grad)


def solution(mesh):
    in_specs = (
        P(("dp", "expert"), None),
        P(("dp", "expert"), None),
        P(("dp", "expert"), None),
        P("dp", "expert", None, "etp"),
        P("expert", "etp", "dp"),
    )
    out_specs = (
        P("expert", "etp", "dp"),
        P("dp", "expert", None, "etp"),
        P(("dp", "expert"), None),
    )
    return jax.shard_map(body, mesh=mesh, in_specs=in_specs, out_specs=out_specs, check_vma=False)
```

```python
import jax
import jax.numpy as jnp
from jax import lax
from jax.sharding import PartitionSpec as P


def body(grad_out, routes, gates, hidden_saved, down_weight):
    token_count = grad_out.shape[0]
    top_count = routes.shape[1]
    exp_dev, ff_part, quarter = down_weight.shape
    groups = lax.axis_size("dp")
    senders = lax.axis_size("expert")
    slot_rows_all = hidden_saved.shape[2]
    capacity = slot_rows_all // senders
    experts = exp_dev * senders
    quarter_cols = grad_out.shape[1] // groups
    meta = jnp.concatenate([routes.astype(grad_out.dtype), gates.astype(grad_out.dtype)], axis=1)
    packed = jnp.concatenate(
        [
            grad_out.reshape(token_count, groups, quarter_cols),
            jnp.broadcast_to(meta[:, None, :], (token_count, groups, 2 * top_count)),
        ],
        axis=2,
    )
    moved = lax.all_to_all(packed, "dp", split_axis=1, concat_axis=0, tiled=True)
    hidden_saved, moved = lax.optimization_barrier((hidden_saved, moved))
    columns = moved[:, 0, :quarter_cols]
    all_meta = moved[:, 0, quarter_cols:]
    hidden_all = lax.all_gather(hidden_saved, "dp", axis=0, tiled=True)
    all_routes = all_meta[:, :top_count].astype(jnp.int32)
    all_gates = all_meta[:, top_count:].astype(gates.dtype)
    pair_count = token_count * top_count
    pair_routes = all_routes.reshape(groups, pair_count)
    expert_ids = jnp.arange(experts, dtype=jnp.int32)
    onehot = (pair_routes[:, :, None] == expert_ids[None, None, :]).astype(jnp.bfloat16)
    pair_ids = jnp.arange(pair_count, dtype=jnp.int32)
    earlier = (pair_ids[:, None] > pair_ids[None, :]).astype(jnp.bfloat16)
    before = jnp.einsum("jk,gke->gje", earlier, onehot, preferred_element_type=jnp.float32)
    slot_ids = jnp.sum(before * onehot.astype(jnp.float32), axis=2).astype(jnp.int32)
    rows = exp_dev * senders * capacity
    position = (pair_routes % exp_dev * senders + pair_routes // exp_dev) * capacity + slot_ids
    position = position.reshape(groups, token_count, top_count)
    row_ids = jnp.arange(rows, dtype=jnp.int32)
    select = (position[..., None] == row_ids).astype(jnp.bfloat16)
    gate_rows = all_gates.reshape(groups, token_count, top_count).astype(jnp.float32)
    gate_table = jnp.einsum("gtk,gtkr->gr", gate_rows, select.astype(jnp.float32))
    token_select = jnp.sum(select, axis=2)
    token_select = token_select.reshape(groups, token_count, exp_dev, senders, capacity)
    token_columns = columns.reshape(groups, token_count, quarter)
    gate_table = (
        gate_table.reshape(groups, exp_dev, senders, capacity).transpose(1, 0, 2, 3).astype(gates.dtype)
    )
    got_gates = lax.all_to_all(gate_table, "expert", split_axis=2, concat_axis=2, tiled=True)
    got_gates = got_gates.reshape(exp_dev, groups, slot_rows_all)
    slot_gates = got_gates.astype(jnp.float32)
    me = lax.axis_index("dp")
    own_gates = lax.dynamic_index_in_dim(got_gates, me, 1, keepdims=False).astype(jnp.float32)
    chunks = 2 if exp_dev % 2 == 0 else 1
    per = exp_dev // chunks
    grads, dots, hidden_parts = [], [], []
    for c in range(chunks):
        local = slice(c * per, (c + 1) * per)
        picked = jnp.einsum(
            "gtlqs,gtd->qglsd",
            token_select[:, :, local],
            token_columns,
            preferred_element_type=jnp.float32,
        ).astype(columns.dtype)
        received = lax.all_to_all(picked, "expert", split_axis=0, concat_axis=0, tiled=True)
        partial = jnp.einsum(
            "qglsd,lfd->glqsf", received, down_weight[local], preferred_element_type=jnp.float32
        ).reshape(groups, per, slot_rows_all, ff_part)
        if c == chunks - 1:
            hidden_all, partial = lax.optimization_barrier((hidden_all, partial))
        sent = partial.astype(jnp.bfloat16)
        arrivals = []
        for shift in range(1, groups):
            chunk = lax.dynamic_index_in_dim(sent, (me + shift) % groups, 0, keepdims=False)
            pairs = [(i, (i + shift) % groups) for i in range(groups)]
            arrivals.append(lax.ppermute(chunk, "dp", pairs))
        hidden_rows = hidden_all[:, local].astype(jnp.float32)
        dots.append(jnp.sum(hidden_rows * partial, axis=3))
        scaled = (jnp.moveaxis(slot_gates[local], 0, 1)[..., None] * hidden_rows).astype(jnp.bfloat16)
        scaled = scaled.reshape(groups, per, senders, capacity, ff_part)
        weight_sum = jnp.einsum("glqsf,qglsd->lfd", scaled, received, preferred_element_type=jnp.float32)
        grads.append(weight_sum.astype(jnp.bfloat16))
        expert_grad = lax.dynamic_index_in_dim(partial, me, 0, keepdims=False)
        if c == chunks - 1:
            weight_grad = jnp.concatenate(grads, axis=0)
            own_select = lax.dynamic_index_in_dim(select, me, 0, keepdims=False).astype(jnp.float32)
            weight_grad, expert_grad, own_select = lax.optimization_barrier(
                (weight_grad, expert_grad, own_select)
            )
        for arrived in arrivals:
            expert_grad = expert_grad + arrived.astype(jnp.float32)
        hidden_parts.append((own_gates[local][..., None] * expert_grad).astype(jnp.bfloat16))
    dot_part = jnp.concatenate(dots, axis=1)
    hidden_grad = jnp.concatenate(hidden_parts, axis=0)[None]
    halves = lax.axis_size("etp")
    half_dots = dot_part
    for shift in range(1, halves):
        pairs = [(i, (i + shift) % halves) for i in range(halves)]
        dot_part = dot_part + lax.ppermute(half_dots, "etp", pairs)
    own_dots = jnp.sum(lax.all_to_all(dot_part, "dp", split_axis=0, concat_axis=0, tiled=True), axis=0)
    hidden_grad, own_dots, weight_grad = lax.optimization_barrier((hidden_grad, own_dots, weight_grad))
    slot_dots = own_dots.reshape(exp_dev, senders, capacity)
    returned = lax.all_to_all(slot_dots, "expert", split_axis=1, concat_axis=1, tiled=True)
    gate_grad = jnp.sum(own_select * returned.reshape(1, 1, rows), axis=2)
    return (weight_grad, hidden_grad, gate_grad)


def solution(mesh):
    in_specs = (
        P(("dp", "expert"), None),
        P(("dp", "expert"), None),
        P(("dp", "expert"), None),
        P("dp", "expert", None, "etp"),
        P("expert", "etp", "dp"),
    )
    out_specs = (
        P("expert", "etp", "dp"),
        P("dp", "expert", None, "etp"),
        P(("dp", "expert"), None),
    )
    return jax.shard_map(body, mesh=mesh, in_specs=in_specs, out_specs=out_specs, check_vma=False)
```
